32 devices in a mesh: sub: 8 (over y, x, core), grp: 4 (over z).
Axes of the slice: x: 2, y: 2, z: 4, core: 2. Of those that a mesh axis runs over, the one named last changes fastest.
Arguments:
- gaps: float32 [4, 16, 96, 1024], P('grp', 'sub'), may hold values from -6 to 6
- dual_op: bfloat16 [4, 16, 1024, 1024], P('grp', 'sub'), may hold values from -1 to 2.5, as said below
- dirichlet: bfloat16 [4, 16, 1024, 1024], P('grp', 'sub'), may hold values from -1 to 2.5, as said below
- modes: float32 [4, 16, 6, 1024], P('grp', 'sub'), may hold values from -6 to 6
- coarse_op: float32 [4, 16, 6, 384], P('grp', 'sub'), may hold values from -0.0009765625 to 0.0009765625, as said below
- slot_map: int32 [4, 16, 1024], P('grp', 'sub'), may hold values from 0 to 1023, as said below
Outputs:
- multipliers: float32 [4, 16, 96, 1024], P('grp', 'sub')
- residual: float32 [4, 16, 96, 1024], P('grp', 'sub')
The draws below stay inside these ranges and needn't reach their ends.
Inputs may be any that keep to these rules, and one draw needn't show every extreme that they name: `dual_op`: each subdomain's block is symmetric positive definite. `dirichlet`: each subdomain's block is symmetric positive definite. The 384 x 384 matrix whose row (16 y + x) * 6 + k is coarse_op[y, x, k] is symmetric. `slot_map`: for every subdomain and face f, the entries f * 256 to (f + 1) * 256 - 1 are a permutation of those same slot numbers.
All inputs are finite; a program needn't handle non-finite values.
Results may differ from the reference program's by a relative error of at most 0.012.
The reference program's roundings to bfloat16 on the way count: a program that leaves them out, or rounds other values in their place, can miss the bound.
Values sent between devices are 32-bit elements; how exact they have to be, the bound alone decides.
No kernel may reach another device: no remote copies, remote signals or barrier semaphores. Data moves between devices by JAX's collectives and lax.ppermute only.
A program may use at most 128 MiB of HBM per device.

```python
import jax
import jax.numpy as jnp
from jax import lax

M = 1024
MODES = 6
NVEC = 96
ITERS = 2
FACE = 256
SUBS_X = 16
SUBS_Y = 4


def draw_gaps(key, part):
    shape_full = (SUBS_Y, SUBS_X, NVEC, M)
    ramp_x = jnp.arange(SUBS_X, dtype=jnp.float32) / max(SUBS_X - 1, 1)
    ramp_y = jnp.arange(SUBS_Y, dtype=jnp.float32) / max(SUBS_Y - 1, 1)
    position = 0.5 * (ramp_x[None, :] + ramp_y[:, None])
    scales = 0.3 * 3.0 ** position
    values = jnp.clip(jax.random.normal(key, shape_full), -6.0, 6.0) * scales[:, :, None, None]
    return values.astype(jnp.float32)


def symmetric_blocks(key, count, order, diag_low, diag_high, spread):
    keys = jax.random.split(key, count)
    factor = spread / (2.0 * order ** 0.5) / 2.0 ** 0.5

    def single(subkey):
        noise_key, diag_key = jax.random.split(subkey)
        noise = jax.random.normal(noise_key, (order, order))
        symmetric = (noise + noise.T) * factor
        diagonal = jnp.exp(jax.random.uniform(diag_key, (order,), minval=jnp.log(diag_low), maxval=jnp.log(diag_high)))
        return (symmetric + jnp.diag(diagonal)).astype(jnp.bfloat16)
    return lax.map(single, keys)


def draw_dual_op(key, part):
    blocks = symmetric_blocks(jax.random.fold_in(key, 3), SUBS_Y * SUBS_X, M, 1.0, 2.0, 0.45)
    return blocks.reshape(SUBS_Y, SUBS_X, M, M)


def draw_dirichlet(key, part):
    blocks = symmetric_blocks(jax.random.fold_in(key, 7), SUBS_Y * SUBS_X, M, 1.0, 2.0, 0.45)
    return blocks.reshape(SUBS_Y, SUBS_X, M, M)


def draw_coarse_op(key, part):
    count = SUBS_Y * SUBS_X * MODES
    noise_key, diag_key = jax.random.split(jax.random.fold_in(key, 5))
    noise = jax.random.normal(noise_key, (count, count))
    symmetric = (noise + noise.T) * (0.3 / (2.0 * count ** 0.5) / 2.0 ** 0.5)
    diagonal = jnp.exp(jax.random.uniform(diag_key, (count,), minval=jnp.log(0.6), maxval=jnp.log(1.2)))
    matrix = (symmetric + jnp.diag(diagonal)) / (2.0 * M)
    return matrix.reshape(SUBS_Y, SUBS_X, MODES, count).astype(jnp.float32)


def draw_slot_map(key, part):
    quarter = M // 4
    keys = jax.random.split(jax.random.fold_in(key, 9), SUBS_Y * SUBS_X * 4)
    perms = jax.vmap(lambda subkey: jax.random.permutation(subkey, quarter))(keys)
    offsets = (jnp.arange(4, dtype=jnp.int32) * quarter)[None, None, :, None]
    perms = perms.astype(jnp.int32).reshape(SUBS_Y, SUBS_X, 4, quarter) + offsets
    return perms.reshape(SUBS_Y, SUBS_X, M).astype(jnp.int32)


def level_of(rng, shape, shards, smallest, high):
    level = 1.0
    for dim, shards_of in shards:
        steps = jax.random.uniform(jax.random.fold_in(jax.random.fold_in(rng, 6), dim), (shards_of,), jnp.float32, smallest / len(shards), high / len(shards))
        level = level * jnp.repeat(jnp.exp(steps), shape[dim] // shards_of).reshape((-1,) + (1,) * (len(shape) - 1 - dim))
    return level


def scatter_about(rng, extent, scale, most, pieces=(), kind=jnp.bfloat16):
    array = jax.random.normal(rng, extent, jnp.float32) * scale
    if len(pieces) > 0:
        array = level_of(rng, extent, pieces, -0.22, 0.18) * array
    return jnp.clip(array, min=-most, max=most).astype(kind)


def setup_inputs(seed: int = 0) -> dict:
    streams_of = jax.random.split(jax.random.key(seed), 7)
    return {
        "gaps": draw_gaps(jax.random.fold_in(streams_of[6], 71), 0),
        "dual_op": draw_dual_op(jax.random.fold_in(streams_of[6], 71), 0),
        "dirichlet": draw_dirichlet(jax.random.fold_in(streams_of[6], 71), 0),
        "modes": scatter_about(streams_of[3], (SUBS_Y, SUBS_X, MODES, M), 1.0, 6.0, ((0, 4), (1, 8)), jnp.float32),
        "coarse_op": draw_coarse_op(jax.random.fold_in(streams_of[6], 71), 0),
        "slot_map": draw_slot_map(jax.random.fold_in(streams_of[6], 71), 0),
    }


HIGHEST = lax.Precision.HIGHEST


def inverse_map(slot_map):
    width = slot_map.shape[-1]
    flattened = slot_map.reshape(-1, width)

    def invert(perm_row):
        return jnp.zeros_like(perm_row).at[perm_row].set(jnp.arange(width, dtype=jnp.int32))

    return jax.vmap(invert)(flattened).reshape(slot_map.shape)


def jump(values, slot_map, back_map):
    total_y, total_x, columns, width = values.shape
    ordered = jnp.take_along_axis(values, slot_map[:, :, None, :], axis=3)
    faces = ordered.reshape(total_y, total_x, columns, 4, width // 4)
    zero_x = jnp.zeros_like(faces[:, :1, :, 0])
    zero_y = jnp.zeros_like(faces[:1, :, :, 0])
    from_left = jnp.concatenate([zero_x, faces[:, :-1, :, 1]], axis=1)
    from_right = jnp.concatenate([faces[:, 1:, :, 0], zero_x], axis=1)
    from_below = jnp.concatenate([zero_y, faces[:-1, :, :, 3]], axis=0)
    from_above = jnp.concatenate([faces[1:, :, :, 2], zero_y], axis=0)
    partner = jnp.stack([from_left, from_right, from_below, from_above], axis=3)
    jumped = (faces - partner).reshape(total_y, total_x, columns, width)
    return jnp.take_along_axis(jumped, back_map[:, :, None, :], axis=3)


def slot_weights():
    x_pos = jnp.arange(SUBS_X, dtype=jnp.int32)
    y_pos = jnp.arange(SUBS_Y, dtype=jnp.int32)
    one = jnp.float32(1.0)
    two = jnp.float32(2.0)
    shape_grid = (SUBS_Y, SUBS_X)
    left_side = jnp.broadcast_to(jnp.where(x_pos == 0, one, two)[None, :], shape_grid)
    right_side = jnp.broadcast_to(jnp.where(x_pos == SUBS_X - 1, one, two)[None, :], shape_grid)
    lower_side = jnp.broadcast_to(jnp.where(y_pos == 0, one, two)[:, None], shape_grid)
    upper_side = jnp.broadcast_to(jnp.where(y_pos == SUBS_Y - 1, one, two)[:, None], shape_grid)
    stacked = jnp.stack([left_side, right_side, lower_side, upper_side], axis=2)
    return jnp.repeat(stacked, FACE, axis=2)


def apply_blocks(values, matrices):
    total_y, total_x, columns, width = values.shape
    rounded = values.astype(jnp.bfloat16).reshape(total_y * total_x, columns, width)
    blocks = matrices.reshape(total_y * total_x, width, width)

    def single(pair):
        return jnp.dot(pair[0], pair[1], preferred_element_type=jnp.float32)

    result = lax.map(single, (rounded, blocks))
    return result.reshape(total_y, total_x, columns, width)


def project(values, modes, weights, coarse_op, slot_map, back_map):
    total_y, total_x, columns, width = values.shape
    weighted = modes * weights[:, :, None, :]
    coefficients = jnp.einsum('yxkm,yxnm->yxkn', weighted, values, precision=HIGHEST)
    stacked = coefficients.reshape(total_y * total_x * MODES, columns)
    amounts = jnp.dot(coarse_op.reshape(-1, stacked.shape[0]), stacked, precision=HIGHEST,
                      preferred_element_type=jnp.float32)
    amounts = amounts.reshape(total_y, total_x, MODES, columns)
    lifted = jnp.einsum('yxkm,yxkn->yxnm', modes, amounts, precision=HIGHEST)
    return values - jump(lifted, slot_map, back_map)


def reference(gaps, dual_op, dirichlet, modes, coarse_op, slot_map):
    back_map = inverse_map(slot_map)
    weights = slot_weights()
    dual = jump(gaps, slot_map, back_map)
    multipliers = jnp.zeros_like(dual)
    residual = project(dual, modes, weights, coarse_op, slot_map, back_map)
    direction = jnp.zeros_like(dual)
    rho_prev = jnp.ones((dual.shape[2],), jnp.float32)
    for step_index in range(ITERS):
        projected = project(residual, modes, weights, coarse_op, slot_map, back_map)
        precond = jump(apply_blocks(projected, dirichlet), slot_map, back_map)
        rho_now = jnp.sum(projected * precond, axis=(0, 1, 3))
        search = project(precond, modes, weights, coarse_op, slot_map, back_map)
        if step_index > 0:
            search = search + (rho_now / rho_prev)[None, None, :, None] * direction
        direction = search
        image = jump(apply_blocks(direction, dual_op), slot_map, back_map)
        curvature = jnp.sum(direction * image, axis=(0, 1, 3))
        step_len = (rho_now / curvature)[None, None, :, None]
        multipliers = multipliers + step_len * direction
        residual = residual - step_len * image
        rho_prev = rho_now
    return multipliers, residual
```

```python
import jax
import jax.numpy as jnp
from jax import lax
from jax.sharding import PartitionSpec as P

MODES = 6
ITERS = 2


HIGHEST = lax.Precision.HIGHEST


def neighbors(d0, d1, d2, d3):
    sub_count = lax.axis_size("sub")
    grp_count = lax.axis_size("grp")
    up_sub = [(i, i + 1) for i in range(sub_count - 1)]
    down_sub = [(i + 1, i) for i in range(sub_count - 1)]
    up_grp = [(i, i + 1) for i in range(grp_count - 1)]
    down_grp = [(i + 1, i) for i in range(grp_count - 1)]
    left_dev = lax.ppermute(d1[-1:], "sub", up_sub)
    right_dev = lax.ppermute(d0[:1], "sub", down_sub)
    from_left = jnp.concatenate([left_dev, d1[:-1]], axis=0)
    from_right = jnp.concatenate([d0[1:], right_dev], axis=0)
    from_below = lax.ppermute(d3, "grp", up_grp)
    from_above = lax.ppermute(d2, "grp", down_grp)
    return jnp.stack([from_left, from_right, from_below, from_above], axis=1)


def face_split(values):
    quarter = values.shape[-1] // 4
    return [values[..., g * quarter:(g + 1) * quarter] for g in range(4)]


def inverse_map(maps):
    width = maps.shape[-1]

    def invert(perm_row):
        return jnp.zeros_like(perm_row).at[perm_row].set(jnp.arange(width, dtype=jnp.int32))

    return jax.vmap(invert)(maps)


def apply_blocks(values, matrices):
    return jnp.einsum(
        "snm,smk->snk", values.astype(jnp.bfloat16), matrices, preferred_element_type=jnp.float32
    )


def shards(gaps, dual_op, dirichlet, modes, coarse_op, slot_map):
    maps = slot_map[0]
    back_map = inverse_map(maps)
    vectors = gaps[0]
    stiffness = dual_op[0]
    schur_blocks = dirichlet[0]
    own_modes = modes[0]
    subdomains, columns, width = vectors.shape
    quarter = width // 4
    sub_total = lax.axis_size("sub")
    grp_total = lax.axis_size("grp")
    x_position = lax.axis_index("sub") * subdomains + jnp.arange(subdomains, dtype=jnp.int32)
    grp_here = lax.axis_index("grp")
    filler = jnp.ones((subdomains,), jnp.float32)
    face_weight = jnp.stack(
        [
            jnp.where(x_position == 0, 1.0, 2.0) * filler,
            jnp.where(x_position == sub_total * subdomains - 1, 1.0, 2.0) * filler,
            jnp.where(grp_here == 0, 1.0, 2.0) * filler,
            jnp.where(grp_here == grp_total - 1, 1.0, 2.0) * filler,
        ],
        axis=1,
    )
    slot_weight = jnp.repeat(face_weight, quarter, axis=1)
    weighted_modes = own_modes * slot_weight[:, None, :]
    rows_here = coarse_op[0].reshape(subdomains * MODES, -1)
    coarse_total = rows_here.shape[1]

    mode_faces = face_split(own_modes)
    map_faces = face_split(maps.astype(jnp.float32)[:, None, :])
    own_rows = coarse_op[0]
    packs = [
        jnp.concatenate(
            [
                mode_faces[g].reshape(subdomains, -1),
                map_faces[g].reshape(subdomains, -1),
                own_rows.reshape(subdomains, -1),
            ],
            axis=1,
        )
        for g in range(4)
    ]
    partner_pack = neighbors(*packs)
    partner_raw_modes = partner_pack[:, :, : MODES * quarter].reshape(subdomains, 4, MODES, quarter)
    partner_map = partner_pack[:, :, MODES * quarter:(MODES + 1) * quarter]
    partner_rows = partner_pack[:, :, (MODES + 1) * quarter:].reshape(
        subdomains, 4, MODES, coarse_total
    )

    opposite = jnp.array([1, 0, 3, 2], jnp.int32)
    local_multiplier = back_map.reshape(subdomains, 4, quarter) - (
        jnp.arange(4, dtype=jnp.int32) * quarter
    )[None, :, None]
    partner_slot = jnp.take_along_axis(
        partner_map.astype(jnp.int32), local_multiplier, axis=2
    ) - (opposite * quarter)[None, :, None]
    permutes = (
        jnp.arange(quarter, dtype=jnp.int32)[None, None, :, None] == partner_slot[:, :, None, :]
    ).astype(jnp.float32)

    def to_mine(raw):
        return jnp.einsum("sfcq,sfqr->sfcr", raw, permutes, precision=HIGHEST)

    partner_modes = to_mine(partner_raw_modes)

    def jump(values):
        raw = neighbors(*face_split(values))
        partner = to_mine(raw)
        partner = jnp.moveaxis(partner, 1, 2).reshape(values.shape)
        return values - partner

    def coefficients(values):
        return jnp.einsum("skm,snm->skn", weighted_modes, values, precision=HIGHEST)

    def gathered(coeffs, extra):
        payload = jnp.concatenate([coeffs.reshape(-1), extra.reshape(-1)])
        everything = lax.all_gather(payload, ("grp", "sub"), axis=0)
        count = coeffs.size
        extras = jnp.sum(everything[:, count:], axis=0)
        if count == 0:
            return None, extras
        flat = everything[:, :count].reshape(-1, columns)
        return flat, extras

    def lift(flat):
        amounts = jnp.dot(rows_here, flat, precision=HIGHEST, preferred_element_type=jnp.float32)
        shaped = amounts.reshape(subdomains, MODES, columns)
        own_part = jnp.einsum("skm,skn->snm", own_modes, shaped, precision=HIGHEST)
        far_amounts = jnp.einsum("sfkc,cn->sfkn", partner_rows, flat, precision=HIGHEST)
        far_part = jnp.einsum("sfkm,sfkn->snfm", partner_modes, far_amounts, precision=HIGHEST)
        return own_part - far_part.reshape(subdomains, columns, width)

    def project_with(values, flat):
        return values - lift(flat)

    nothing = jnp.zeros((1,), jnp.float32)
    dual = jump(vectors)
    flat_dual, _ = gathered(coefficients(dual), nothing)
    residual = project_with(dual, flat_dual)
    flat_residual, _ = gathered(coefficients(residual), nothing)
    multipliers = jnp.zeros_like(dual)
    direction = jnp.zeros_like(dual)
    rho_prev = jnp.ones((columns,), jnp.float32)
    for step_index in range(ITERS):
        projected = project_with(residual, flat_residual)
        precond = jump(apply_blocks(projected, schur_blocks))
        flat_precond, rho_now = gathered(
            coefficients(precond), jnp.sum(projected * precond, axis=(0, 2))
        )
        search = project_with(precond, flat_precond)
        if step_index > 0:
            search = search + (rho_now / rho_prev)[None, :, None] * direction
        direction = search
        image = jump(apply_blocks(direction, stiffness))
        partial_dot = jnp.sum(direction * image, axis=(0, 2))
        if step_index + 1 < ITERS:
            flat_image, curvature = gathered(coefficients(image), partial_dot)
        else:
            _, curvature = gathered(jnp.zeros((0,), jnp.float32), partial_dot)
        step_len = rho_now / curvature
        multipliers = multipliers + step_len[None, :, None] * direction
        residual = residual - step_len[None, :, None] * image
        if step_index + 1 < ITERS:
            flat_residual = flat_residual - step_len[None, :] * flat_image
        rho_prev = rho_now
    return (multipliers[None], residual[None])


def solution(mesh):
    placed = (
        P("grp", "sub", None, None),
        P("grp", "sub", None, None),
        P("grp", "sub", None, None),
        P("grp", "sub", None, None),
        P("grp", "sub", None, None),
        P("grp", "sub", None),
    )
    return jax.shard_map(
        shards,
        mesh=mesh,
        in_specs=placed,
        out_specs=(P("grp", "sub", None, None), P("grp", "sub", None, None)),
        check_vma=False,
    )
```

```python
import jax
import jax.numpy as jnp
from jax import lax
from jax.sharding import PartitionSpec as P

MODES = 6
ITERS = 2


HIGHEST = lax.Precision.HIGHEST


def neighbors(d0, d1, d2, d3):
    sub_count = lax.axis_size("sub")
    grp_count = lax.axis_size("grp")
    up_sub = [(i, i + 1) for i in range(sub_count - 1)]
    down_sub = [(i + 1, i) for i in range(sub_count - 1)]
    up_grp = [(i, i + 1) for i in range(grp_count - 1)]
    down_grp = [(i + 1, i) for i in range(grp_count - 1)]
    left_dev = lax.ppermute(d1[-1:], "sub", up_sub)
    right_dev = lax.ppermute(d0[:1], "sub", down_sub)
    from_left = jnp.concatenate([left_dev, d1[:-1]], axis=0)
    from_right = jnp.concatenate([d0[1:], right_dev], axis=0)
    from_below = lax.ppermute(d3, "grp", up_grp)
    from_above = lax.ppermute(d2, "grp", down_grp)
    return jnp.stack([from_left, from_right, from_below, from_above], axis=1)


def face_split(values):
    quarter = values.shape[-1] // 4
    return [values[..., g * quarter:(g + 1) * quarter] for g in range(4)]


def apply_blocks(values, matrices):
    return jnp.einsum(
        "snm,smk->snk", values.astype(jnp.bfloat16), matrices, preferred_element_type=jnp.float32
    )


def shards(gaps, dual_op, dirichlet, modes, coarse_op, slot_map):
    maps = slot_map[0]
    vectors = gaps[0]
    stiffness = dual_op[0]
    schur_blocks = dirichlet[0]
    own_modes = modes[0]
    subdomains, columns, width = vectors.shape
    quarter = width // 4
    sub_total = lax.axis_size("sub")
    grp_total = lax.axis_size("grp")
    x_position = lax.axis_index("sub") * subdomains + jnp.arange(subdomains, dtype=jnp.int32)
    grp_here = lax.axis_index("grp")
    filler = jnp.ones((subdomains,), jnp.float32)
    face_weight = jnp.stack(
        [
            jnp.where(x_position == 0, 1.0, 2.0) * filler,
            jnp.where(x_position == sub_total * subdomains - 1, 1.0, 2.0) * filler,
            jnp.where(grp_here == 0, 1.0, 2.0) * filler,
            jnp.where(grp_here == grp_total - 1, 1.0, 2.0) * filler,
        ],
        axis=1,
    )
    slot_weight = jnp.repeat(face_weight, quarter, axis=1)
    weighted_modes = own_modes * slot_weight[:, None, :]
    rows_here = coarse_op[0].reshape(subdomains * MODES, -1)
    coarse_total = rows_here.shape[1]

    mode_faces = face_split(own_modes)
    map_faces = face_split(maps.astype(jnp.float32)[:, None, :])
    own_rows = coarse_op[0]
    packs = [
        jnp.concatenate(
            [
                mode_faces[g].reshape(subdomains, -1),
                map_faces[g].reshape(subdomains, -1),
                own_rows.reshape(subdomains, -1),
            ],
            axis=1,
        )
        for g in range(4)
    ]
    partner_pack = neighbors(*packs)
    partner_raw_modes = partner_pack[:, :, : MODES * quarter].reshape(subdomains, 4, MODES, quarter)
    partner_map = partner_pack[:, :, MODES * quarter:(MODES + 1) * quarter]
    partner_rows = partner_pack[:, :, (MODES + 1) * quarter:].reshape(
        subdomains, 4, MODES, coarse_total
    )

    opposite = jnp.array([1, 0, 3, 2], jnp.int32)
    offsets = (jnp.arange(4, dtype=jnp.int32) * quarter)[None, :, None]
    my_slot = maps.reshape(subdomains, 4, quarter) - offsets
    partner_slot = partner_map.astype(jnp.int32) - (opposite * quarter)[None, :, None]
    local = jnp.arange(quarter, dtype=jnp.int32)[None, None, None, :]
    mine_hot = (my_slot[..., None] == local).astype(jnp.bfloat16)
    partner_hot = (partner_slot[..., None] == local).astype(jnp.bfloat16)
    permutes = jnp.einsum(
        "sfmt,sfmi->sfti", partner_hot, mine_hot, preferred_element_type=jnp.float32
    )

    def to_mine(raw):
        return jnp.einsum("sfcq,sfqr->sfcr", raw, permutes, precision=HIGHEST)

    partner_modes = to_mine(partner_raw_modes)

    def jump(values):
        raw = neighbors(*face_split(values))
        partner = to_mine(raw)
        partner = jnp.moveaxis(partner, 1, 2).reshape(values.shape)
        return values - partner

    def coefficients(values):
        return jnp.einsum("skm,snm->skn", weighted_modes, values, precision=HIGHEST)

    def gathered(coeffs, extra):
        payload = jnp.concatenate([coeffs.reshape(-1), extra.reshape(-1)])
        devices = lax.axis_size("grp") * lax.axis_size("sub")
        copies = jnp.broadcast_to(payload[None], (devices, payload.shape[0]))
        everything = lax.all_to_all(copies, ("grp", "sub"), 0, 0, tiled=True)
        count = coeffs.size
        extras = jnp.sum(everything[:, count:], axis=0)
        if count == 0:
            return None, extras
        flat = everything[:, :count].reshape(-1, columns)
        return flat, extras

    def lift(flat):
        amounts = jnp.dot(rows_here, flat, precision=HIGHEST, preferred_element_type=jnp.float32)
        shaped = amounts.reshape(subdomains, MODES, columns)
        own_part = jnp.einsum("skm,skn->snm", own_modes, shaped, precision=HIGHEST)
        far_amounts = jnp.einsum("sfkc,cn->sfkn", partner_rows, flat, precision=HIGHEST)
        far_part = jnp.einsum("sfkm,sfkn->snfm", partner_modes, far_amounts, precision=HIGHEST)
        return own_part - far_part.reshape(subdomains, columns, width)

    def project_with(values, flat):
        return values - lift(flat)

    nothing = jnp.zeros((1,), jnp.float32)
    dual = jump(vectors)
    flat_dual, _ = gathered(coefficients(dual), nothing)
    residual = project_with(dual, flat_dual)
    flat_residual, _ = gathered(coefficients(residual), nothing)
    multipliers = jnp.zeros_like(dual)
    direction = jnp.zeros_like(dual)
    rho_prev = jnp.ones((columns,), jnp.float32)
    for step_index in range(ITERS):
        projected = project_with(residual, flat_residual)
        precond = jump(apply_blocks(projected, schur_blocks))
        flat_precond, rho_now = gathered(
            coefficients(precond), jnp.sum(projected * precond, axis=(0, 2))
        )
        search = project_with(precond, flat_precond)
        if step_index > 0:
            search = search + (rho_now / rho_prev)[None, :, None] * direction
        direction = search
        image = jump(apply_blocks(direction, stiffness))
        partial_dot = jnp.sum(direction * image, axis=(0, 2))
        if step_index + 1 < ITERS:
            flat_image, curvature = gathered(coefficients(image), partial_dot)
        else:
            _, curvature = gathered(jnp.zeros((0,), jnp.float32), partial_dot)
        step_len = rho_now / curvature
        multipliers = multipliers + step_len[None, :, None] * direction
        residual = residual - step_len[None, :, None] * image
        if step_index + 1 < ITERS:
            flat_residual = flat_residual - step_len[None, :] * flat_image
        rho_prev = rho_now
    return (multipliers[None], residual[None])


def solution(mesh):
    placed = (
        P("grp", "sub", None, None),
        P("grp", "sub", None, None),
        P("grp", "sub", None, None),
        P("grp", "sub", None, None),
        P("grp", "sub", None, None),
        P("grp", "sub", None),
    )
    return jax.shard_map(
        shards,
        mesh=mesh,
        in_specs=placed,
        out_specs=(P("grp", "sub", None, None), P("grp", "sub", None, None)),
        check_vma=False,
    )
```

```python
import jax
import jax.numpy as jnp
from jax import lax
from jax.sharding import PartitionSpec as P

MODES = 6
ITERS = 2


HIGHEST = lax.Precision.HIGHEST


def neighbors(d0, d1, d2, d3):
    sub_count = lax.axis_size("sub")
    grp_count = lax.axis_size("grp")
    up_sub = [(i, i + 1) for i in range(sub_count - 1)]
    down_sub = [(i + 1, i) for i in range(sub_count - 1)]
    up_grp = [(i, i + 1) for i in range(grp_count - 1)]
    down_grp = [(i + 1, i) for i in range(grp_count - 1)]
    left_dev = lax.ppermute(d1[-1:], "sub", up_sub)
    right_dev = lax.ppermute(d0[:1], "sub", down_sub)
    from_left = jnp.concatenate([left_dev, d1[:-1]], axis=0)
    from_right = jnp.concatenate([d0[1:], right_dev], axis=0)
    from_below = lax.ppermute(d3, "grp", up_grp)
    from_above = lax.ppermute(d2, "grp", down_grp)
    return jnp.stack([from_left, from_right, from_below, from_above], axis=1)


def face_split(values):
    quarter = values.shape[-1] // 4
    return [values[..., g * quarter:(g + 1) * quarter] for g in range(4)]


def apply_blocks(values, matrices):
    return jnp.einsum(
        "snm,smk->snk", values.astype(jnp.bfloat16), matrices, preferred_element_type=jnp.float32
    )


def shards(gaps, dual_op, dirichlet, modes, coarse_op, slot_map):
    maps = slot_map[0]
    vectors = gaps[0]
    stiffness = dual_op[0]
    schur_blocks = dirichlet[0]
    own_modes = modes[0]
    subdomains, columns, width = vectors.shape
    quarter = width // 4
    sub_total = lax.axis_size("sub")
    grp_total = lax.axis_size("grp")
    x_position = lax.axis_index("sub") * subdomains + jnp.arange(subdomains, dtype=jnp.int32)
    grp_here = lax.axis_index("grp")
    filler = jnp.ones((subdomains,), jnp.float32)
    face_weight = jnp.stack(
        [
            jnp.where(x_position == 0, 1.0, 2.0) * filler,
            jnp.where(x_position == sub_total * subdomains - 1, 1.0, 2.0) * filler,
            jnp.where(grp_here == 0, 1.0, 2.0) * filler,
            jnp.where(grp_here == grp_total - 1, 1.0, 2.0) * filler,
        ],
        axis=1,
    )
    slot_weight = jnp.repeat(face_weight, quarter, axis=1)
    weighted_modes = own_modes * slot_weight[:, None, :]
    rows_here = coarse_op[0].reshape(subdomains * MODES, -1)
    coarse_total = rows_here.shape[1]

    gap_faces = face_split(vectors)
    mode_faces = face_split(own_modes)
    map_faces = face_split(maps.astype(jnp.float32)[:, None, :])
    own_rows = coarse_op[0]
    gap_size = columns * quarter
    packs = [
        jnp.concatenate(
            [
                gap_faces[g].reshape(subdomains, -1),
                mode_faces[g].reshape(subdomains, -1),
                map_faces[g].reshape(subdomains, -1),
                own_rows.reshape(subdomains, -1),
            ],
            axis=1,
        )
        for g in range(4)
    ]
    partner_pack = neighbors(*packs)
    partner_gaps = partner_pack[:, :, :gap_size].reshape(subdomains, 4, columns, quarter)
    partner_pack = partner_pack[:, :, gap_size:]
    partner_raw_modes = partner_pack[:, :, : MODES * quarter].reshape(subdomains, 4, MODES, quarter)
    partner_map = partner_pack[:, :, MODES * quarter:(MODES + 1) * quarter]
    partner_rows = partner_pack[:, :, (MODES + 1) * quarter:].reshape(
        subdomains, 4, MODES, coarse_total
    )

    opposite = jnp.array([1, 0, 3, 2], jnp.int32)
    offsets = (jnp.arange(4, dtype=jnp.int32) * quarter)[None, :, None]
    my_slot = maps.reshape(subdomains, 4, quarter) - offsets
    partner_slot = partner_map.astype(jnp.int32) - (opposite * quarter)[None, :, None]
    local = jnp.arange(quarter, dtype=jnp.int32)[None, None, None, :]
    mine_hot = (my_slot[..., None] == local).astype(jnp.bfloat16)
    partner_hot = (partner_slot[..., None] == local).astype(jnp.bfloat16)
    permutes = jnp.einsum(
        "sfmt,sfmi->sfti", partner_hot, mine_hot, preferred_element_type=jnp.float32
    )

    def to_mine(raw):
        return jnp.einsum("sfcq,sfqr->sfcr", raw, permutes, precision=HIGHEST)

    partner_modes = to_mine(partner_raw_modes)
    partner_weighted = partner_modes * slot_weight.reshape(subdomains, 4, 1, quarter)

    def partner_values(raw, shape):
        return jnp.moveaxis(to_mine(raw), 1, 2).reshape(shape)

    def coefficients(values):
        return jnp.einsum("skm,snm->skn", weighted_modes, values, precision=HIGHEST)

    def gathered(payload):
        devices = lax.axis_size("grp") * lax.axis_size("sub")
        copies = jnp.broadcast_to(payload[None], (devices, payload.shape[0]))
        return lax.all_to_all(copies, ("grp", "sub"), 0, 0, tiled=True)

    block = MODES * columns

    def jump_and_gather(product, partial, with_coefficients=True):
        raw = neighbors(*face_split(product))
        if with_coefficients:
            own = coefficients(product)
            faces = product.reshape(subdomains, columns, 4, quarter)
            given = jnp.einsum(
                "sfkq,snfq->sfkn", partner_weighted, faces, precision=HIGHEST
            )
            zero = jnp.zeros_like(own[:1])
            own = own - jnp.concatenate([zero, given[:-1, 1]], axis=0)
            own = own - jnp.concatenate([given[1:, 0], zero], axis=0)
            pieces = [own, given[0, 0], given[-1, 1], given[:, 2], given[:, 3]]
            payload = jnp.concatenate([p.reshape(-1) for p in pieces] + [partial])
        else:
            payload = partial
        everything = gathered(payload)
        total = jnp.sum(everything[:, payload.shape[0] - columns:], axis=0)
        jumped = product - partner_values(raw, product.shape)
        if not with_coefficients:
            return jumped, None, total
        flat = coefficient_table(everything)
        return jumped, flat, total

    def coefficient_table(everything):
        shape = (grp_total, sub_total)
        cursor = 0

        def take(count, tail):
            nonlocal cursor
            piece = everything[:, cursor:cursor + count].reshape(shape + tail)
            cursor += count
            return piece

        own = take(subdomains * block, (subdomains, MODES, columns))
        to_left = take(block, (MODES, columns))
        to_right = take(block, (MODES, columns))
        to_below = take(subdomains * block, (subdomains, MODES, columns))
        to_above = take(subdomains * block, (subdomains, MODES, columns))
        from_left = jnp.pad(to_right, ((0, 0), (1, 0), (0, 0), (0, 0)))[:, :-1]
        from_right = jnp.pad(to_left, ((0, 0), (0, 1), (0, 0), (0, 0)))[:, 1:]
        from_below = jnp.pad(to_above, ((1, 0), (0, 0), (0, 0), (0, 0), (0, 0)))[:-1]
        from_above = jnp.pad(to_below, ((0, 1), (0, 0), (0, 0), (0, 0), (0, 0)))[1:]
        edge_first = (jnp.arange(subdomains) == 0)[:, None, None]
        edge_last = (jnp.arange(subdomains) == subdomains - 1)[:, None, None]
        table = own - from_below - from_above
        table = table - jnp.where(edge_first, from_left[:, :, None], 0.0)
        table = table - jnp.where(edge_last, from_right[:, :, None], 0.0)
        return table.reshape(-1, columns)

    def lift(flat):
        amounts = jnp.dot(rows_here, flat, precision=HIGHEST, preferred_element_type=jnp.float32)
        shaped = amounts.reshape(subdomains, MODES, columns)
        own_part = jnp.einsum("skm,skn->snm", own_modes, shaped, precision=HIGHEST)
        far_amounts = jnp.einsum("sfkc,cn->sfkn", partner_rows, flat, precision=HIGHEST)
        far_part = jnp.einsum("sfkm,sfkn->snfm", partner_modes, far_amounts, precision=HIGHEST)
        return own_part - far_part.reshape(subdomains, columns, width)

    def project_with(values, flat):
        return values - lift(flat)

    def coefficients_everywhere(values):
        payload = coefficients(values).reshape(-1)
        return gathered(payload).reshape(-1, columns)

    dual = vectors - partner_values(partner_gaps, vectors.shape)
    flat_dual = coefficients_everywhere(dual)
    residual = project_with(dual, flat_dual)
    flat_residual = coefficients_everywhere(residual)
    multipliers = jnp.zeros_like(dual)
    direction = jnp.zeros_like(dual)
    rho_prev = jnp.ones((columns,), jnp.float32)
    weight_column = slot_weight[:, None, :]
    for step_index in range(ITERS):
        projected = project_with(residual, flat_residual)
        product = apply_blocks(projected, schur_blocks)
        rho_part = jnp.sum(weight_column * projected * product, axis=(0, 2))
        precond, flat_precond, rho_now = jump_and_gather(product, rho_part)
        search = project_with(precond, flat_precond)
        if step_index > 0:
            search = search + (rho_now / rho_prev)[None, :, None] * direction
        direction = search
        product = apply_blocks(direction, stiffness)
        curv_part = jnp.sum(weight_column * direction * product, axis=(0, 2))
        last = step_index + 1 == ITERS
        image, flat_image, curvature = jump_and_gather(product, curv_part, not last)
        step_len = rho_now / curvature
        multipliers = multipliers + step_len[None, :, None] * direction
        residual = residual - step_len[None, :, None] * image
        if not last:
            flat_residual = flat_residual - step_len[None, :] * flat_image
        rho_prev = rho_now
    return (multipliers[None], residual[None])


def solution(mesh):
    placed = (
        P("grp", "sub", None, None),
        P("grp", "sub", None, None),
        P("grp", "sub", None, None),
        P("grp", "sub", None, None),
        P("grp", "sub", None, None),
        P("grp", "sub", None),
    )
    return jax.shard_map(
        shards,
        mesh=mesh,
        in_specs=placed,
        out_specs=(P("grp", "sub", None, None), P("grp", "sub", None, None)),
        check_vma=False,
    )
```

```python
import jax
import jax.numpy as jnp
from jax import lax
from jax.sharding import PartitionSpec as P

MODES = 6
ROWS = 8
ITERS = 2


HIGHEST = lax.Precision.HIGHEST


def neighbors(d0, d1, d2, d3):
    sub_count = lax.axis_size("sub")
    grp_count = lax.axis_size("grp")
    up_sub = [(i, i + 1) for i in range(sub_count - 1)]
    down_sub = [(i + 1, i) for i in range(sub_count - 1)]
    up_grp = [(i, i + 1) for i in range(grp_count - 1)]
    down_grp = [(i + 1, i) for i in range(grp_count - 1)]
    left_dev = lax.ppermute(d1[-1:], "sub", up_sub)
    right_dev = lax.ppermute(d0[:1], "sub", down_sub)
    from_left = jnp.concatenate([left_dev, d1[:-1]], axis=0)
    from_right = jnp.concatenate([d0[1:], right_dev], axis=0)
    from_below = lax.ppermute(d3, "grp", up_grp)
    from_above = lax.ppermute(d2, "grp", down_grp)
    return jnp.stack([from_left, from_right, from_below, from_above], axis=1)


def face_split(values):
    quarter = values.shape[-1] // 4
    return [values[..., g * quarter:(g + 1) * quarter] for g in range(4)]


def apply_blocks(values, matrices):
    return jnp.einsum(
        "snm,smk->snk", values.astype(jnp.bfloat16), matrices, preferred_element_type=jnp.float32
    )


def shards(gaps, dual_op, dirichlet, modes, coarse_op, slot_map):
    maps = slot_map[0]
    vectors = gaps[0]
    stiffness = dual_op[0]
    schur_blocks = dirichlet[0]
    own_modes = modes[0]
    subdomains, columns, width = vectors.shape
    quarter = width // 4
    sub_total = lax.axis_size("sub")
    grp_total = lax.axis_size("grp")
    x_position = lax.axis_index("sub") * subdomains + jnp.arange(subdomains, dtype=jnp.int32)
    grp_here = lax.axis_index("grp")
    filler = jnp.ones((subdomains,), jnp.float32)
    face_weight = jnp.stack(
        [
            jnp.where(x_position == 0, 1.0, 2.0) * filler,
            jnp.where(x_position == sub_total * subdomains - 1, 1.0, 2.0) * filler,
            jnp.where(grp_here == 0, 1.0, 2.0) * filler,
            jnp.where(grp_here == grp_total - 1, 1.0, 2.0) * filler,
        ],
        axis=1,
    )
    slot_weight = jnp.repeat(face_weight, quarter, axis=1)
    weighted_modes = own_modes * slot_weight[:, None, :]
    padding = ROWS - MODES
    weighted_padded = jnp.pad(weighted_modes, ((0, 0), (0, padding), (0, 0)))
    rows_here = coarse_op[0].reshape(subdomains * MODES, -1)
    coarse_total = rows_here.shape[1]
    subdomain_count = coarse_total // MODES

    def pad_columns(rows):
        lead = rows.shape[:-1]
        split = rows.reshape(lead + (subdomain_count, MODES))
        widths = [(0, 0)] * len(lead) + [(0, 0), (0, padding)]
        return jnp.pad(split, widths).reshape(lead + (subdomain_count * ROWS,))

    rows_padded = pad_columns(rows_here)

    gap_faces = face_split(vectors)
    mode_faces = face_split(own_modes)
    map_faces = face_split(maps.astype(jnp.float32)[:, None, :])
    own_rows = coarse_op[0]
    gap_size = columns * quarter
    packs = [
        jnp.concatenate(
            [
                gap_faces[g].reshape(subdomains, -1),
                mode_faces[g].reshape(subdomains, -1),
                map_faces[g].reshape(subdomains, -1),
                own_rows.reshape(subdomains, -1),
            ],
            axis=1,
        )
        for g in range(4)
    ]
    partner_pack = neighbors(*packs)
    partner_gaps = partner_pack[:, :, :gap_size].reshape(subdomains, 4, columns, quarter)
    partner_pack = partner_pack[:, :, gap_size:]
    partner_raw_modes = partner_pack[:, :, : MODES * quarter].reshape(subdomains, 4, MODES, quarter)
    partner_map = partner_pack[:, :, MODES * quarter:(MODES + 1) * quarter]
    partner_rows = partner_pack[:, :, (MODES + 1) * quarter:].reshape(
        subdomains, 4, MODES, coarse_total
    )

    opposite = jnp.array([1, 0, 3, 2], jnp.int32)
    offsets = (jnp.arange(4, dtype=jnp.int32) * quarter)[None, :, None]
    my_slot = maps.reshape(subdomains, 4, quarter) - offsets
    partner_slot = partner_map.astype(jnp.int32) - (opposite * quarter)[None, :, None]
    local = jnp.arange(quarter, dtype=jnp.int32)[None, None, None, :]
    mine_hot = (my_slot[..., None] == local).astype(jnp.bfloat16)
    partner_hot = (partner_slot[..., None] == local).astype(jnp.bfloat16)
    permutes = jnp.einsum(
        "sfmt,sfmi->sfti", partner_hot, mine_hot, preferred_element_type=jnp.float32
    )

    def to_mine(raw):
        return jnp.einsum("sfcq,sfqr->sfcr", raw, permutes, precision=HIGHEST)

    partner_modes = to_mine(partner_raw_modes)
    partner_weighted = partner_modes * slot_weight.reshape(subdomains, 4, 1, quarter)
    partner_weighted = jnp.pad(partner_weighted, ((0, 0), (0, 0), (0, padding), (0, 0)))
    partner_rows_padded = pad_columns(partner_rows)

    def partner_values(raw, shape):
        return jnp.moveaxis(to_mine(raw), 1, 2).reshape(shape)

    def coefficients(values):
        return jnp.einsum("skm,snm->skn", weighted_padded, values, precision=HIGHEST)

    def gathered(payload):
        devices = lax.axis_size("grp") * lax.axis_size("sub")
        copies = jnp.broadcast_to(payload[None], (devices,) + payload.shape)
        everything = lax.all_to_all(copies, ("grp", "sub"), 0, 0, tiled=True)
        return everything.reshape((grp_total, sub_total) + payload.shape)

    band = subdomains * ROWS

    def jump_and_gather(product, partial, with_coefficients=True):
        raw = neighbors(*face_split(product))
        partial_rows = jnp.pad(partial[None], ((0, ROWS - 1), (0, 0)))
        if with_coefficients:
            own = coefficients(product)
            faces = product.reshape(subdomains, columns, 4, quarter)
            given = jnp.einsum(
                "sfkq,snfq->sfkn", partner_weighted, faces, precision=HIGHEST
            )
            zero = jnp.zeros_like(own[:1])
            own = own - jnp.concatenate([zero, given[:-1, 1]], axis=0)
            own = own - jnp.concatenate([given[1:, 0], zero], axis=0)
            pieces = [own, given[:1, 0], given[-1:, 1], given[:, 2], given[:, 3]]
            payload = jnp.concatenate(
                [p.reshape(-1, columns) for p in pieces] + [partial_rows], axis=0
            )
        else:
            payload = partial_rows
        everything = gathered(payload)
        total = jnp.sum(everything[:, :, -ROWS], axis=(0, 1))
        jumped = product - partner_values(raw, product.shape)
        if not with_coefficients:
            return jumped, None, total
        return jumped, coefficient_table(everything), total

    def coefficient_table(everything):
        own = everything[:, :, :band]
        to_left = everything[:, :, band:band + ROWS]
        to_right = everything[:, :, band + ROWS:band + 2 * ROWS]
        to_below = everything[:, :, band + 2 * ROWS:2 * band + 2 * ROWS]
        to_above = everything[:, :, 2 * band + 2 * ROWS:3 * band + 2 * ROWS]
        no_x = ((0, 0), (0, 0), (0, 0))
        from_left = jnp.pad(to_right, ((0, 0), (1, 0)) + no_x[1:])[:, :-1]
        from_right = jnp.pad(to_left, ((0, 0), (0, 1)) + no_x[1:])[:, 1:]
        from_below = jnp.pad(to_above, ((1, 0),) + no_x)[:-1]
        from_above = jnp.pad(to_below, ((0, 1),) + no_x)[1:]
        rest = ((0, 0), (0, 0))
        first = jnp.pad(from_left, rest + ((0, band - ROWS), (0, 0)))
        last = jnp.pad(from_right, rest + ((band - ROWS, 0), (0, 0)))
        table = own - from_below - from_above - first - last
        return table.reshape(-1, columns)

    def lift(flat):
        amounts = jnp.dot(rows_padded, flat, precision=HIGHEST, preferred_element_type=jnp.float32)
        shaped = amounts.reshape(subdomains, MODES, columns)
        own_part = jnp.einsum("skm,skn->snm", own_modes, shaped, precision=HIGHEST)
        far_amounts = jnp.einsum("sfkc,cn->sfkn", partner_rows_padded, flat, precision=HIGHEST)
        far_part = jnp.einsum("sfkm,sfkn->snfm", partner_modes, far_amounts, precision=HIGHEST)
        return own_part - far_part.reshape(subdomains, columns, width)

    def project_with(values, flat):
        return values - lift(flat)

    def coefficients_everywhere(values):
        payload = coefficients(values).reshape(-1, columns)
        return gathered(payload).reshape(-1, columns)

    dual = vectors - partner_values(partner_gaps, vectors.shape)
    flat_dual = coefficients_everywhere(dual)
    residual = project_with(dual, flat_dual)
    flat_residual = coefficients_everywhere(residual)
    multipliers = jnp.zeros_like(dual)
    direction = jnp.zeros_like(dual)
    rho_prev = jnp.ones((columns,), jnp.float32)
    weight_column = slot_weight[:, None, :]
    for step_index in range(ITERS):
        projected = project_with(residual, flat_residual)
        product = apply_blocks(projected, schur_blocks)
        rho_part = jnp.sum(weight_column * projected * product, axis=(0, 2))
        precond, flat_precond, rho_now = jump_and_gather(product, rho_part)
        search = project_with(precond, flat_precond)
        if step_index > 0:
            search = search + (rho_now / rho_prev)[None, :, None] * direction
        direction = search
        product = apply_blocks(direction, stiffness)
        curv_part = jnp.sum(weight_column * direction * product, axis=(0, 2))
        last = step_index + 1 == ITERS
        image, flat_image, curvature = jump_and_gather(product, curv_part, not last)
        step_len = rho_now / curvature
        multipliers = multipliers + step_len[None, :, None] * direction
        residual = residual - step_len[None, :, None] * image
        if not last:
            flat_residual = flat_residual - step_len[None, :] * flat_image
        rho_prev = rho_now
    return (multipliers[None], residual[None])


def solution(mesh):
    placed = (
        P("grp", "sub", None, None),
        P("grp", "sub", None, None),
        P("grp", "sub", None, None),
        P("grp", "sub", None, None),
        P("grp", "sub", None, None),
        P("grp", "sub", None),
    )
    return jax.shard_map(
        shards,
        mesh=mesh,
        in_specs=placed,
        out_specs=(P("grp", "sub", None, None), P("grp", "sub", None, None)),
        check_vma=False,
    )
```

```python
import jax
import jax.numpy as jnp
from jax import lax
from jax.sharding import PartitionSpec as P

MODES = 6
ITERS = 2


HIGHEST = lax.Precision.HIGHEST


def neighbors(d0, d1, d2, d3):
    sub_count = lax.axis_size("sub")
    grp_count = lax.axis_size("grp")
    up_sub = [(i, i + 1) for i in range(sub_count - 1)]
    down_sub = [(i + 1, i) for i in range(sub_count - 1)]
    up_grp = [(i, i + 1) for i in range(grp_count - 1)]
    down_grp = [(i + 1, i) for i in range(grp_count - 1)]
    left_dev = lax.ppermute(d1[-1:], "sub", up_sub)
    right_dev = lax.ppermute(d0[:1], "sub", down_sub)
    from_left = jnp.concatenate([left_dev, d1[:-1]], axis=0)
    from_right = jnp.concatenate([d0[1:], right_dev], axis=0)
    from_below = lax.ppermute(d3, "grp", up_grp)
    from_above = lax.ppermute(d2, "grp", down_grp)
    return jnp.stack([from_left, from_right, from_below, from_above], axis=1)


def face_split(values):
    quarter = values.shape[-1] // 4
    return [values[..., g * quarter:(g + 1) * quarter] for g in range(4)]


def apply_blocks(values, matrices):
    return jnp.einsum(
        "snm,smk->snk", values.astype(jnp.bfloat16), matrices, preferred_element_type=jnp.float32
    )


def shards(gaps, dual_op, dirichlet, modes, coarse_op, slot_map):
    maps = slot_map[0]
    vectors = gaps[0]
    stiffness = dual_op[0]
    schur_blocks = dirichlet[0]
    own_modes = modes[0]
    subdomains, columns, width = vectors.shape
    quarter = width // 4
    sub_total = lax.axis_size("sub")
    grp_total = lax.axis_size("grp")
    x_position = lax.axis_index("sub") * subdomains + jnp.arange(subdomains, dtype=jnp.int32)
    grp_here = lax.axis_index("grp")
    filler = jnp.ones((subdomains,), jnp.float32)
    face_weight = jnp.stack(
        [
            jnp.where(x_position == 0, 1.0, 2.0) * filler,
            jnp.where(x_position == sub_total * subdomains - 1, 1.0, 2.0) * filler,
            jnp.where(grp_here == 0, 1.0, 2.0) * filler,
            jnp.where(grp_here == grp_total - 1, 1.0, 2.0) * filler,
        ],
        axis=1,
    )
    slot_weight = jnp.repeat(face_weight, quarter, axis=1)
    weighted_modes = own_modes * slot_weight[:, None, :]
    rows_here = coarse_op[0].reshape(subdomains * MODES, -1)
    coarse_total = rows_here.shape[1]

    gap_faces = face_split(vectors)
    mode_faces = face_split(own_modes)
    map_faces = face_split(maps.astype(jnp.float32)[:, None, :])
    own_rows = coarse_op[0]
    gap_size = columns * quarter
    packs = [
        jnp.concatenate(
            [
                gap_faces[g].reshape(subdomains, -1),
                mode_faces[g].reshape(subdomains, -1),
                map_faces[g].reshape(subdomains, -1),
                own_rows.reshape(subdomains, -1),
            ],
            axis=1,
        )
        for g in range(4)
    ]
    partner_pack = neighbors(*packs)
    partner_gaps = partner_pack[:, :, :gap_size].reshape(subdomains, 4, columns, quarter)
    partner_pack = partner_pack[:, :, gap_size:]
    partner_raw_modes = partner_pack[:, :, : MODES * quarter].reshape(subdomains, 4, MODES, quarter)
    partner_map = partner_pack[:, :, MODES * quarter:(MODES + 1) * quarter]
    partner_rows = partner_pack[:, :, (MODES + 1) * quarter:].reshape(
        subdomains, 4, MODES, coarse_total
    )

    opposite = jnp.array([1, 0, 3, 2], jnp.int32)
    offsets = (jnp.arange(4, dtype=jnp.int32) * quarter)[None, :, None]
    my_slot = maps.reshape(subdomains, 4, quarter) - offsets
    partner_slot = partner_map.astype(jnp.int32) - (opposite * quarter)[None, :, None]
    local = jnp.arange(quarter, dtype=jnp.int32)[None, None, None, :]
    mine_hot = (my_slot[..., None] == local).astype(jnp.bfloat16)
    partner_hot = (partner_slot[..., None] == local).astype(jnp.bfloat16)
    permutes = jnp.einsum(
        "sfmt,sfmi->sfti", partner_hot, mine_hot, preferred_element_type=jnp.float32
    )

    def to_mine(raw):
        return jnp.einsum("sfcq,sfqr->sfcr", raw, permutes, precision=HIGHEST)

    partner_modes = to_mine(partner_raw_modes)

    def partner_values(raw, shape):
        return jnp.moveaxis(to_mine(raw), 1, 2).reshape(shape)

    def jump(values):
        raw = neighbors(*face_split(values))
        return values - partner_values(raw, values.shape)

    def coefficients(values):
        return jnp.einsum("skm,snm->skn", weighted_modes, values, precision=HIGHEST)

    def gathered(coeffs, extra):
        payload = jnp.concatenate([coeffs.reshape(-1), extra.reshape(-1)])
        devices = lax.axis_size("grp") * lax.axis_size("sub")
        copies = jnp.broadcast_to(payload[None], (devices, payload.shape[0]))
        everything = lax.all_to_all(copies, ("grp", "sub"), 0, 0, tiled=True)
        count = coeffs.size
        extras = jnp.sum(everything[:, count:], axis=0)
        if count == 0:
            return None, extras
        flat = everything[:, :count].reshape(-1, columns)
        return flat, extras

    def lift(flat):
        amounts = jnp.dot(rows_here, flat, precision=HIGHEST, preferred_element_type=jnp.float32)
        shaped = amounts.reshape(subdomains, MODES, columns)
        own_part = jnp.einsum("skm,skn->snm", own_modes, shaped, precision=HIGHEST)
        far_amounts = jnp.einsum("sfkc,cn->sfkn", partner_rows, flat, precision=HIGHEST)
        far_part = jnp.einsum("sfkm,sfkn->snfm", partner_modes, far_amounts, precision=HIGHEST)
        return own_part - far_part.reshape(subdomains, columns, width)

    def project_with(values, flat):
        return values - lift(flat)

    nothing = jnp.zeros((1,), jnp.float32)
    dual = vectors - partner_values(partner_gaps, vectors.shape)
    flat_dual, _ = gathered(coefficients(dual), nothing)
    residual = project_with(dual, flat_dual)
    flat_residual, _ = gathered(coefficients(residual), nothing)
    multipliers = jnp.zeros_like(dual)
    direction = jnp.zeros_like(dual)
    rho_prev = jnp.ones((columns,), jnp.float32)
    for step_index in range(ITERS):
        projected = project_with(residual, flat_residual)
        precond = jump(apply_blocks(projected, schur_blocks))
        flat_precond, rho_now = gathered(
            coefficients(precond), jnp.sum(projected * precond, axis=(0, 2))
        )
        search = project_with(precond, flat_precond)
        if step_index > 0:
            search = search + (rho_now / rho_prev)[None, :, None] * direction
        direction = search
        image = jump(apply_blocks(direction, stiffness))
        partial_dot = jnp.sum(direction * image, axis=(0, 2))
        if step_index + 1 < ITERS:
            flat_image, curvature = gathered(coefficients(image), partial_dot)
        else:
            _, curvature = gathered(jnp.zeros((0,), jnp.float32), partial_dot)
        step_len = rho_now / curvature
        multipliers = multipliers + step_len[None, :, None] * direction
        residual = residual - step_len[None, :, None] * image
        if step_index + 1 < ITERS:
            flat_residual = flat_residual - step_len[None, :] * flat_image
        rho_prev = rho_now
    return (multipliers[None], residual[None])


def solution(mesh):
    placed = (
        P("grp", "sub", None, None),
        P("grp", "sub", None, None),
        P("grp", "sub", None, None),
        P("grp", "sub", None, None),
        P("grp", "sub", None, None),
        P("grp", "sub", None),
    )
    return jax.shard_map(
        shards,
        mesh=mesh,
        in_specs=placed,
        out_specs=(P("grp", "sub", None, None), P("grp", "sub", None, None)),
        check_vma=False,
    )
```

```python
import jax
import jax.numpy as jnp
from jax import lax
from jax.sharding import PartitionSpec as P

MODES = 6
ITERS = 2


HIGHEST = lax.Precision.HIGHEST


def neighbors(d0, d1, d2, d3):
    sub_count = lax.axis_size("sub")
    grp_count = lax.axis_size("grp")
    up_sub = [(i, i + 1) for i in range(sub_count - 1)]
    down_sub = [(i + 1, i) for i in range(sub_count - 1)]
    up_grp = [(i, i + 1) for i in range(grp_count - 1)]
    down_grp = [(i + 1, i) for i in range(grp_count - 1)]
    left_dev = lax.ppermute(d1[-1:], "sub", up_sub)
    right_dev = lax.ppermute(d0[:1], "sub", down_sub)
    from_left = jnp.concatenate([left_dev, d1[:-1]], axis=0)
    from_right = jnp.concatenate([d0[1:], right_dev], axis=0)
    from_below = lax.ppermute(d3, "grp", up_grp)
    from_above = lax.ppermute(d2, "grp", down_grp)
    return jnp.stack([from_left, from_right, from_below, from_above], axis=1)


def face_split(values):
    quarter = values.shape[-1] // 4
    return [values[..., g * quarter:(g + 1) * quarter] for g in range(4)]


def apply_blocks(values, matrices):
    return jnp.einsum(
        "snm,smk->snk", values.astype(jnp.bfloat16), matrices, preferred_element_type=jnp.float32
    )


def shards(gaps, dual_op, dirichlet, modes, coarse_op, slot_map):
    maps = slot_map[0]
    vectors = gaps[0]
    stiffness = dual_op[0]
    schur_blocks = dirichlet[0]
    own_modes = modes[0]
    subdomains, columns, width = vectors.shape
    quarter = width // 4
    sub_total = lax.axis_size("sub")
    grp_total = lax.axis_size("grp")
    x_position = lax.axis_index("sub") * subdomains + jnp.arange(subdomains, dtype=jnp.int32)
    grp_here = lax.axis_index("grp")
    filler = jnp.ones((subdomains,), jnp.float32)
    face_weight = jnp.stack(
        [
            jnp.where(x_position == 0, 1.0, 2.0) * filler,
            jnp.where(x_position == sub_total * subdomains - 1, 1.0, 2.0) * filler,
            jnp.where(grp_here == 0, 1.0, 2.0) * filler,
            jnp.where(grp_here == grp_total - 1, 1.0, 2.0) * filler,
        ],
        axis=1,
    )
    slot_weight = jnp.repeat(face_weight, quarter, axis=1)
    weighted_modes = own_modes * slot_weight[:, None, :]
    rows_here = coarse_op[0].reshape(subdomains * MODES, -1)
    coarse_total = rows_here.shape[1]

    gap_faces = face_split(vectors)
    mode_faces = face_split(own_modes)
    map_faces = face_split(maps.astype(jnp.float32)[:, None, :])
    own_rows = coarse_op[0]
    gap_size = columns * quarter
    packs = [
        jnp.concatenate(
            [
                gap_faces[g].reshape(subdomains, -1),
                mode_faces[g].reshape(subdomains, -1),
                map_faces[g].reshape(subdomains, -1),
                own_rows.reshape(subdomains, -1),
            ],
            axis=1,
        )
        for g in range(4)
    ]
    partner_pack = neighbors(*packs)
    partner_gaps = partner_pack[:, :, :gap_size].reshape(subdomains, 4, columns, quarter)
    partner_pack = partner_pack[:, :, gap_size:]
    partner_raw_modes = partner_pack[:, :, : MODES * quarter].reshape(subdomains, 4, MODES, quarter)
    partner_map = partner_pack[:, :, MODES * quarter:(MODES + 1) * quarter]
    partner_rows = partner_pack[:, :, (MODES + 1) * quarter:].reshape(
        subdomains, 4, MODES, coarse_total
    )

    opposite = jnp.array([1, 0, 3, 2], jnp.int32)
    offsets = (jnp.arange(4, dtype=jnp.int32) * quarter)[None, :, None]
    my_slot = maps.reshape(subdomains, 4, quarter) - offsets
    partner_slot = partner_map.astype(jnp.int32) - (opposite * quarter)[None, :, None]
    local = jnp.arange(quarter, dtype=jnp.int32)[None, None, None, :]
    mine_hot = (my_slot[..., None] == local).astype(jnp.bfloat16)
    partner_hot = (partner_slot[..., None] == local).astype(jnp.bfloat16)
    permutes = jnp.einsum(
        "sfmt,sfmi->sfti", partner_hot, mine_hot, preferred_element_type=jnp.float32
    )

    def to_mine(raw):
        return jnp.einsum("sfcq,sfqr->sfcr", raw, permutes, precision=HIGHEST)

    partner_modes = to_mine(partner_raw_modes)

    def partner_values(raw, shape):
        return jnp.moveaxis(to_mine(raw), 1, 2).reshape(shape)

    def jump(values):
        raw = neighbors(*face_split(values))
        return values - partner_values(raw, values.shape)

    def coefficients(values):
        return jnp.einsum("skm,snm->skn", weighted_modes, values, precision=HIGHEST)

    def gathered(coeffs, extra):
        payload = jnp.concatenate([coeffs.reshape(-1), extra.reshape(-1)])
        devices = lax.axis_size("grp") * lax.axis_size("sub")
        copies = jnp.broadcast_to(payload[None], (devices, payload.shape[0]))
        everything = lax.all_to_all(copies, ("grp", "sub"), 0, 0, tiled=True)
        count = coeffs.size
        extras = jnp.sum(everything[:, count:], axis=0)
        if count == 0:
            return None, extras
        flat = everything[:, :count].reshape(-1, columns)
        return flat, extras

    def lift(flat):
        amounts = jnp.dot(rows_here, flat, precision=HIGHEST, preferred_element_type=jnp.float32)
        shaped = amounts.reshape(subdomains, MODES, columns)
        own_part = jnp.einsum("skm,skn->snm", own_modes, shaped, precision=HIGHEST)
        far_amounts = jnp.einsum("sfkc,cn->sfkn", partner_rows, flat, precision=HIGHEST)
        far_part = jnp.einsum("sfkm,sfkn->snfm", partner_modes, far_amounts, precision=HIGHEST)
        return own_part - far_part.reshape(subdomains, columns, width)

    def project_with(values, flat):
        return values - lift(flat)

    nothing = jnp.zeros((1,), jnp.float32)
    dual = vectors - partner_values(partner_gaps, vectors.shape)
    flat_dual, _ = gathered(coefficients(dual), nothing)
    residual = project_with(dual, flat_dual)
    flat_residual, _ = gathered(coefficients(residual), nothing)
    multipliers = jnp.zeros_like(dual)
    direction = jnp.zeros_like(dual)
    rho_prev = jnp.ones((columns,), jnp.float32)

    def iteration(_, state):
        residual, flat_residual, multipliers, direction, rho_prev = state
        projected = project_with(residual, flat_residual)
        precond = jump(apply_blocks(projected, schur_blocks))
        flat_precond, rho_now = gathered(
            coefficients(precond), jnp.sum(projected * precond, axis=(0, 2))
        )
        search = project_with(precond, flat_precond)
        direction = search + (rho_now / rho_prev)[None, :, None] * direction
        image = jump(apply_blocks(direction, stiffness))
        partial_dot = jnp.sum(direction * image, axis=(0, 2))
        flat_image, curvature = gathered(coefficients(image), partial_dot)
        step_len = rho_now / curvature
        multipliers = multipliers + step_len[None, :, None] * direction
        residual = residual - step_len[None, :, None] * image
        flat_residual = flat_residual - step_len[None, :] * flat_image
        return residual, flat_residual, multipliers, direction, rho_now

    state = (residual, flat_residual, multipliers, direction, rho_prev)
    residual, _, multipliers, _, _ = lax.fori_loop(0, ITERS, iteration, state)
    return (multipliers[None], residual[None])


def solution(mesh):
    placed = (
        P("grp", "sub", None, None),
        P("grp", "sub", None, None),
        P("grp", "sub", None, None),
        P("grp", "sub", None, None),
        P("grp", "sub", None, None),
        P("grp", "sub", None),
    )
    return jax.shard_map(
        shards,
        mesh=mesh,
        in_specs=placed,
        out_specs=(P("grp", "sub", None, None), P("grp", "sub", None, None)),
        check_vma=False,
    )
```

```python
import jax
import jax.numpy as jnp
from jax import lax
from jax.sharding import PartitionSpec as P

MODES = 6
ITERS = 2


HIGHEST = lax.Precision.HIGHEST


def neighbors(d0, d1, d2, d3):
    sub_count = lax.axis_size("sub")
    grp_count = lax.axis_size("grp")
    up_sub = [(i, i + 1) for i in range(sub_count - 1)]
    down_sub = [(i + 1, i) for i in range(sub_count - 1)]
    up_grp = [(i, i + 1) for i in range(grp_count - 1)]
    down_grp = [(i + 1, i) for i in range(grp_count - 1)]
    left_dev = lax.ppermute(d1[-1:], "sub", up_sub)
    right_dev = lax.ppermute(d0[:1], "sub", down_sub)
    from_left = jnp.concatenate([left_dev, d1[:-1]], axis=0)
    from_right = jnp.concatenate([d0[1:], right_dev], axis=0)
    from_below = lax.ppermute(d3, "grp", up_grp)
    from_above = lax.ppermute(d2, "grp", down_grp)
    return jnp.stack([from_left, from_right, from_below, from_above], axis=1)


def face_split(values):
    quarter = values.shape[-1] // 4
    return [values[..., g * quarter:(g + 1) * quarter] for g in range(4)]


def apply_blocks(values, matrices):
    return jnp.einsum(
        "snm,smk->snk", values.astype(jnp.bfloat16), matrices, preferred_element_type=jnp.float32
    )


def shards(gaps, dual_op, dirichlet, modes, coarse_op, slot_map):
    maps = slot_map[0]
    vectors = gaps[0]
    stiffness = dual_op[0]
    schur_blocks = dirichlet[0]
    own_modes = modes[0]
    subdomains, columns, width = vectors.shape
    quarter = width // 4
    sub_total = lax.axis_size("sub")
    grp_total = lax.axis_size("grp")
    x_position = lax.axis_index("sub") * subdomains + jnp.arange(subdomains, dtype=jnp.int32)
    grp_here = lax.axis_index("grp")
    filler = jnp.ones((subdomains,), jnp.float32)
    face_weight = jnp.stack(
        [
            jnp.where(x_position == 0, 1.0, 2.0) * filler,
            jnp.where(x_position == sub_total * subdomains - 1, 1.0, 2.0) * filler,
            jnp.where(grp_here == 0, 1.0, 2.0) * filler,
            jnp.where(grp_here == grp_total - 1, 1.0, 2.0) * filler,
        ],
        axis=1,
    )
    slot_weight = jnp.repeat(face_weight, quarter, axis=1)
    weighted_modes = own_modes * slot_weight[:, None, :]
    rows_here = coarse_op[0].reshape(subdomains * MODES, -1)
    coarse_total = rows_here.shape[1]

    gap_faces = face_split(vectors)
    mode_faces = face_split(own_modes)
    map_faces = face_split(maps.astype(jnp.float32)[:, None, :])
    own_rows = coarse_op[0]
    gap_size = columns * quarter
    packs = [
        jnp.concatenate(
            [
                gap_faces[g].reshape(subdomains, -1),
                mode_faces[g].reshape(subdomains, -1),
                map_faces[g].reshape(subdomains, -1),
                own_rows.reshape(subdomains, -1),
            ],
            axis=1,
        )
        for g in range(4)
    ]
    partner_pack = neighbors(*packs)
    partner_gaps = partner_pack[:, :, :gap_size].reshape(subdomains, 4, columns, quarter)
    partner_pack = partner_pack[:, :, gap_size:]
    partner_raw_modes = partner_pack[:, :, : MODES * quarter].reshape(subdomains, 4, MODES, quarter)
    partner_map = partner_pack[:, :, MODES * quarter:(MODES + 1) * quarter]
    partner_rows = partner_pack[:, :, (MODES + 1) * quarter:].reshape(
        subdomains, 4, MODES, coarse_total
    )

    opposite = jnp.array([1, 0, 3, 2], jnp.int32)
    offsets = (jnp.arange(4, dtype=jnp.int32) * quarter)[None, :, None]
    my_slot = maps.reshape(subdomains, 4, quarter) - offsets
    partner_slot = partner_map.astype(jnp.int32) - (opposite * quarter)[None, :, None]
    local = jnp.arange(quarter, dtype=jnp.int32)[None, None, None, :]
    mine_hot = (my_slot[..., None] == local).astype(jnp.bfloat16)
    partner_hot = (partner_slot[..., None] == local).astype(jnp.bfloat16)
    permutes = jnp.einsum(
        "sfmt,sfmi->sfti", partner_hot, mine_hot, preferred_element_type=jnp.float32
    )

    def to_mine(raw):
        return jnp.einsum("sfcq,sfqr->sfcr", raw, permutes, precision=HIGHEST)

    partner_modes = to_mine(partner_raw_modes)

    def partner_values(raw, shape):
        return jnp.moveaxis(to_mine(raw), 1, 2).reshape(shape)

    def jump(values):
        raw = neighbors(*face_split(values))
        return values - partner_values(raw, values.shape)

    def coefficients(values):
        return jnp.einsum("skm,snm->skn", weighted_modes, values, precision=HIGHEST)

    def gathered(coeffs, extra, rider=None):
        riders = [] if rider is None else [rider]
        payload = jnp.concatenate([coeffs.reshape(-1), extra.reshape(-1)] + riders)
        devices = lax.axis_size("grp") * lax.axis_size("sub")
        copies = jnp.broadcast_to(payload[None], (devices, payload.shape[0]))
        everything = lax.all_to_all(copies, ("grp", "sub"), 0, 0, tiled=True)
        count = coeffs.size
        ends = count + extra.size
        extras = jnp.sum(everything[:, count:ends], axis=0)
        if count == 0:
            return None, extras
        flat = everything[:, :count].reshape(-1, columns)
        if rider is not None:
            return flat, extras, everything[:, ends:]
        return flat, extras

    def lift(flat):
        amounts = jnp.dot(rows_here, flat, precision=HIGHEST, preferred_element_type=jnp.float32)
        shaped = amounts.reshape(subdomains, MODES, columns)
        own_part = jnp.einsum("skm,skn->snm", own_modes, shaped, precision=HIGHEST)
        far_amounts = jnp.einsum("sfkc,cn->sfkn", partner_rows, flat, precision=HIGHEST)
        far_part = jnp.einsum("sfkm,sfkn->snfm", partner_modes, far_amounts, precision=HIGHEST)
        return own_part - far_part.reshape(subdomains, columns, width)

    def project_with(values, flat):
        return values - lift(flat)

    by_grp = lax.all_gather(coarse_op[0], "grp", axis=0)
    coarse_full = lax.all_gather(by_grp, "sub", axis=1).reshape(coarse_total, coarse_total)
    self_coupling = jnp.einsum("skm,sjm->skj", weighted_modes, own_modes, precision=HIGHEST)
    face_weighted = weighted_modes.reshape(subdomains, MODES, 4, quarter)
    face_coupling = jnp.einsum(
        "skfq,sfjq->sfkj", face_weighted, partner_modes, precision=HIGHEST
    )
    couplings = jnp.concatenate([self_coupling.reshape(-1), face_coupling.reshape(-1)])

    nothing = jnp.zeros((1,), jnp.float32)
    dual = vectors - partner_values(partner_gaps, vectors.shape)
    flat_dual, _, coupling_all = gathered(coefficients(dual), nothing, couplings)
    residual = project_with(dual, flat_dual)
    grid = (grp_total, sub_total * subdomains)
    couple_self = coupling_all[:, : subdomains * MODES * MODES].reshape(grid + (MODES, MODES))
    couple_face = coupling_all[:, subdomains * MODES * MODES:].reshape(
        (grp_total, sub_total, subdomains, 4, MODES, MODES)
    ).reshape(grid + (4, MODES, MODES))
    amounts_all = jnp.dot(coarse_full, flat_dual, precision=HIGHEST)
    amounts_all = amounts_all.reshape(grid + (MODES, columns))
    no_tail = ((0, 0), (0, 0))
    beside = [
        jnp.pad(amounts_all, ((0, 0), (1, 0)) + no_tail)[:, :-1],
        jnp.pad(amounts_all, ((0, 0), (0, 1)) + no_tail)[:, 1:],
        jnp.pad(amounts_all, ((1, 0), (0, 0)) + no_tail)[:-1],
        jnp.pad(amounts_all, ((0, 1), (0, 0)) + no_tail)[1:],
    ]
    lifted_coeffs = jnp.einsum("yxkj,yxjn->yxkn", couple_self, amounts_all, precision=HIGHEST)
    for f in range(4):
        lifted_coeffs = lifted_coeffs - jnp.einsum(
            "yxkj,yxjn->yxkn", couple_face[:, :, f], beside[f], precision=HIGHEST
        )
    flat_residual = flat_dual - lifted_coeffs.reshape(-1, columns)
    multipliers = jnp.zeros_like(dual)
    direction = jnp.zeros_like(dual)
    rho_prev = jnp.ones((columns,), jnp.float32)
    for step_index in range(ITERS):
        projected = project_with(residual, flat_residual)
        precond = jump(apply_blocks(projected, schur_blocks))
        flat_precond, rho_now = gathered(
            coefficients(precond), jnp.sum(projected * precond, axis=(0, 2))
        )
        search = project_with(precond, flat_precond)
        if step_index > 0:
            search = search + (rho_now / rho_prev)[None, :, None] * direction
        direction = search
        image = jump(apply_blocks(direction, stiffness))
        partial_dot = jnp.sum(direction * image, axis=(0, 2))
        if step_index + 1 < ITERS:
            flat_image, curvature = gathered(coefficients(image), partial_dot)
        else:
            _, curvature = gathered(jnp.zeros((0,), jnp.float32), partial_dot)
        step_len = rho_now / curvature
        multipliers = multipliers + step_len[None, :, None] * direction
        residual = residual - step_len[None, :, None] * image
        if step_index + 1 < ITERS:
            flat_residual = flat_residual - step_len[None, :] * flat_image
        rho_prev = rho_now
    return (multipliers[None], residual[None])


def solution(mesh):
    placed = (
        P("grp", "sub", None, None),
        P("grp", "sub", None, None),
        P("grp", "sub", None, None),
        P("grp", "sub", None, None),
        P("grp", "sub", None, None),
        P("grp", "sub", None),
    )
    return jax.shard_map(
        shards,
        mesh=mesh,
        in_specs=placed,
        out_specs=(P("grp", "sub", None, None), P("grp", "sub", None, None)),
        check_vma=False,
    )
```

```python
import jax
import jax.numpy as jnp
from jax import lax
from jax.sharding import PartitionSpec as P

MODES = 6
ROWS = 8
ITERS = 2


HIGHEST = lax.Precision.HIGHEST


def neighbors(d0, d1, d2, d3):
    sub_count = lax.axis_size("sub")
    grp_count = lax.axis_size("grp")
    up_sub = [(i, i + 1) for i in range(sub_count - 1)]
    down_sub = [(i + 1, i) for i in range(sub_count - 1)]
    up_grp = [(i, i + 1) for i in range(grp_count - 1)]
    down_grp = [(i + 1, i) for i in range(grp_count - 1)]
    left_dev = lax.ppermute(d1[-1:], "sub", up_sub)
    right_dev = lax.ppermute(d0[:1], "sub", down_sub)
    from_left = jnp.concatenate([left_dev, d1[:-1]], axis=0)
    from_right = jnp.concatenate([d0[1:], right_dev], axis=0)
    from_below = lax.ppermute(d3, "grp", up_grp)
    from_above = lax.ppermute(d2, "grp", down_grp)
    return jnp.stack([from_left, from_right, from_below, from_above], axis=1)


def face_split(values):
    quarter = values.shape[-1] // 4
    return [values[..., g * quarter:(g + 1) * quarter] for g in range(4)]


def apply_blocks(values, matrices):
    return jnp.einsum(
        "snm,smk->snk", values.astype(jnp.bfloat16), matrices, preferred_element_type=jnp.float32
    )


def shards(gaps, dual_op, dirichlet, modes, coarse_op, slot_map):
    maps = slot_map[0]
    vectors = gaps[0]
    stiffness = dual_op[0]
    schur_blocks = dirichlet[0]
    own_modes = modes[0]
    subdomains, columns, width = vectors.shape
    quarter = width // 4
    sub_total = lax.axis_size("sub")
    grp_total = lax.axis_size("grp")
    x_position = lax.axis_index("sub") * subdomains + jnp.arange(subdomains, dtype=jnp.int32)
    grp_here = lax.axis_index("grp")
    filler = jnp.ones((subdomains,), jnp.float32)
    face_weight = jnp.stack(
        [
            jnp.where(x_position == 0, 1.0, 2.0) * filler,
            jnp.where(x_position == sub_total * subdomains - 1, 1.0, 2.0) * filler,
            jnp.where(grp_here == 0, 1.0, 2.0) * filler,
            jnp.where(grp_here == grp_total - 1, 1.0, 2.0) * filler,
        ],
        axis=1,
    )
    slot_weight = jnp.repeat(face_weight, quarter, axis=1)
    weighted_modes = own_modes * slot_weight[:, None, :]
    padding = ROWS - MODES
    weighted_padded = jnp.pad(weighted_modes, ((0, 0), (0, padding), (0, 0)))
    rows_here = coarse_op[0].reshape(subdomains * MODES, -1)
    coarse_total = rows_here.shape[1]
    subdomain_count = coarse_total // MODES

    def pad_columns(rows):
        lead = rows.shape[:-1]
        split = rows.reshape(lead + (subdomain_count, MODES))
        widths = [(0, 0)] * len(lead) + [(0, 0), (0, padding)]
        return jnp.pad(split, widths).reshape(lead + (subdomain_count * ROWS,))

    rows_padded = pad_columns(rows_here)

    gap_faces = face_split(vectors)
    mode_faces = face_split(own_modes)
    map_faces = face_split(maps.astype(jnp.float32)[:, None, :])
    own_rows = coarse_op[0]
    gap_size = columns * quarter
    packs = [
        jnp.concatenate(
            [
                gap_faces[g].reshape(subdomains, -1),
                mode_faces[g].reshape(subdomains, -1),
                map_faces[g].reshape(subdomains, -1),
                own_rows.reshape(subdomains, -1),
            ],
            axis=1,
        )
        for g in range(4)
    ]
    partner_pack = neighbors(*packs)
    partner_gaps = partner_pack[:, :, :gap_size].reshape(subdomains, 4, columns, quarter)
    partner_pack = partner_pack[:, :, gap_size:]
    partner_raw_modes = partner_pack[:, :, : MODES * quarter].reshape(subdomains, 4, MODES, quarter)
    partner_map = partner_pack[:, :, MODES * quarter:(MODES + 1) * quarter]
    partner_rows = partner_pack[:, :, (MODES + 1) * quarter:].reshape(
        subdomains, 4, MODES, coarse_total
    )

    opposite = jnp.array([1, 0, 3, 2], jnp.int32)
    offsets = (jnp.arange(4, dtype=jnp.int32) * quarter)[None, :, None]
    my_slot = maps.reshape(subdomains, 4, quarter) - offsets
    partner_slot = partner_map.astype(jnp.int32) - (opposite * quarter)[None, :, None]
    local = jnp.arange(quarter, dtype=jnp.int32)[None, None, None, :]
    mine_hot = (my_slot[..., None] == local).astype(jnp.bfloat16)
    partner_hot = (partner_slot[..., None] == local).astype(jnp.bfloat16)
    permutes = jnp.einsum(
        "sfmt,sfmi->sfti", partner_hot, mine_hot, preferred_element_type=jnp.float32
    )

    def to_mine(raw):
        return jnp.einsum("sfcq,sfqr->sfcr", raw, permutes, precision=HIGHEST)

    partner_modes = to_mine(partner_raw_modes)
    partner_slot_modes = jnp.moveaxis(partner_modes, 1, 2).reshape(subdomains, MODES, width)
    partner_rows_padded = pad_columns(partner_rows)

    def partner_values(raw, shape):
        return jnp.moveaxis(to_mine(raw), 1, 2).reshape(shape)

    def jump(values):
        raw = neighbors(*face_split(values))
        return values - partner_values(raw, values.shape)

    def coefficients(values):
        return jnp.einsum("skm,snm->skn", weighted_padded, values, precision=HIGHEST)

    def gathered(coeffs, extra=None):
        pieces = [] if coeffs is None else [coeffs.reshape(-1, columns)]
        if extra is not None:
            pieces.append(jnp.pad(extra[None], ((0, ROWS - 1), (0, 0))))
        payload = jnp.concatenate(pieces, axis=0)
        devices = lax.axis_size("grp") * lax.axis_size("sub")
        copies = jnp.broadcast_to(payload[None], (devices,) + payload.shape)
        everything = lax.all_to_all(copies, ("grp", "sub"), 0, 0, tiled=True)
        extras = None if extra is None else jnp.sum(everything[:, -ROWS], axis=0)
        if coeffs is None:
            return None, extras
        flat = everything[:, : subdomains * ROWS].reshape(-1, columns)
        return flat, extras

    def lift(flat):
        amounts = jnp.dot(rows_padded, flat, precision=HIGHEST, preferred_element_type=jnp.float32)
        shaped = amounts.reshape(subdomains, MODES, columns)
        far_amounts = jnp.einsum(
            "sfkc,cn->skfn", partner_rows_padded, flat, precision=HIGHEST
        )
        far_spread = jnp.repeat(jnp.swapaxes(far_amounts, 2, 3), quarter, axis=3)
        own_part = own_modes[:, :, None, :] * shaped[:, :, :, None]
        far_part = partner_slot_modes[:, :, None, :] * far_spread
        return jnp.sum(own_part - far_part, axis=1)

    def project_with(values, flat):
        return values - lift(flat)

    dual = vectors - partner_values(partner_gaps, vectors.shape)
    flat_dual, _ = gathered(coefficients(dual))
    residual = project_with(dual, flat_dual)
    flat_residual, _ = gathered(coefficients(residual))
    multipliers = jnp.zeros_like(dual)
    direction = jnp.zeros_like(dual)
    rho_prev = jnp.ones((columns,), jnp.float32)
    for step_index in range(ITERS):
        projected = project_with(residual, flat_residual)
        precond = jump(apply_blocks(projected, schur_blocks))
        flat_precond, rho_now = gathered(
            coefficients(precond), jnp.sum(projected * precond, axis=(0, 2))
        )
        search = project_with(precond, flat_precond)
        if step_index > 0:
            search = search + (rho_now / rho_prev)[None, :, None] * direction
        direction = search
        image = jump(apply_blocks(direction, stiffness))
        partial_dot = jnp.sum(direction * image, axis=(0, 2))
        if step_index + 1 < ITERS:
            flat_image, curvature = gathered(coefficients(image), partial_dot)
        else:
            _, curvature = gathered(None, partial_dot)
        step_len = rho_now / curvature
        multipliers = multipliers + step_len[None, :, None] * direction
        residual = residual - step_len[None, :, None] * image
        if step_index + 1 < ITERS:
            flat_residual = flat_residual - step_len[None, :] * flat_image
        rho_prev = rho_now
    return (multipliers[None], residual[None])


def solution(mesh):
    placed = (
        P("grp", "sub", None, None),
        P("grp", "sub", None, None),
        P("grp", "sub", None, None),
        P("grp", "sub", None, None),
        P("grp", "sub", None, None),
        P("grp", "sub", None),
    )
    return jax.shard_map(
        shards,
        mesh=mesh,
        in_specs=placed,
        out_specs=(P("grp", "sub", None, None), P("grp", "sub", None, None)),
        check_vma=False,
    )
```

```python
import jax
import jax.numpy as jnp
from jax import lax
from jax.sharding import PartitionSpec as P

MODES = 6
ITERS = 2


HIGHEST = lax.Precision.HIGHEST


def neighbors(d0, d1, d2, d3):
    sub_count = lax.axis_size("sub")
    grp_count = lax.axis_size("grp")
    up_sub = [(i, i + 1) for i in range(sub_count - 1)]
    down_sub = [(i + 1, i) for i in range(sub_count - 1)]
    up_grp = [(i, i + 1) for i in range(grp_count - 1)]
    down_grp = [(i + 1, i) for i in range(grp_count - 1)]
    left_dev = lax.ppermute(d1[-1:], "sub", up_sub)
    right_dev = lax.ppermute(d0[:1], "sub", down_sub)
    from_left = jnp.concatenate([left_dev, d1[:-1]], axis=0)
    from_right = jnp.concatenate([d0[1:], right_dev], axis=0)
    from_below = lax.ppermute(d3, "grp", up_grp)
    from_above = lax.ppermute(d2, "grp", down_grp)
    return jnp.stack([from_left, from_right, from_below, from_above], axis=1)


def face_split(values):
    quarter = values.shape[-1] // 4
    return [values[..., g * quarter:(g + 1) * quarter] for g in range(4)]


def apply_blocks(values, matrices):
    return jnp.einsum(
        "snm,smk->snk", values.astype(jnp.bfloat16), matrices, preferred_element_type=jnp.float32
    )


def shards(gaps, dual_op, dirichlet, modes, coarse_op, slot_map):
    maps = slot_map[0]
    vectors = gaps[0]
    stiffness = dual_op[0]
    schur_blocks = dirichlet[0]
    own_modes = modes[0]
    subdomains, columns, width = vectors.shape
    quarter = width // 4
    sub_total = lax.axis_size("sub")
    grp_total = lax.axis_size("grp")
    x_position = lax.axis_index("sub") * subdomains + jnp.arange(subdomains, dtype=jnp.int32)
    grp_here = lax.axis_index("grp")
    filler = jnp.ones((subdomains,), jnp.float32)
    face_weight = jnp.stack(
        [
            jnp.where(x_position == 0, 1.0, 2.0) * filler,
            jnp.where(x_position == sub_total * subdomains - 1, 1.0, 2.0) * filler,
            jnp.where(grp_here == 0, 1.0, 2.0) * filler,
            jnp.where(grp_here == grp_total - 1, 1.0, 2.0) * filler,
        ],
        axis=1,
    )
    slot_weight = jnp.repeat(face_weight, quarter, axis=1)
    weighted_modes = own_modes * slot_weight[:, None, :]
    rows_here = coarse_op[0].reshape(subdomains * MODES, -1)
    coarse_total = rows_here.shape[1]

    gap_faces = face_split(vectors)
    mode_faces = face_split(own_modes)
    map_faces = face_split(maps.astype(jnp.float32)[:, None, :])
    own_rows = coarse_op[0]
    gap_size = columns * quarter
    packs = [
        jnp.concatenate(
            [
                gap_faces[g].reshape(subdomains, -1),
                mode_faces[g].reshape(subdomains, -1),
                map_faces[g].reshape(subdomains, -1),
                own_rows.reshape(subdomains, -1),
            ],
            axis=1,
        )
        for g in range(4)
    ]
    partner_pack = neighbors(*packs)
    partner_gaps = partner_pack[:, :, :gap_size].reshape(subdomains, 4, columns, quarter)
    partner_pack = partner_pack[:, :, gap_size:]
    partner_raw_modes = partner_pack[:, :, : MODES * quarter].reshape(subdomains, 4, MODES, quarter)
    partner_map = partner_pack[:, :, MODES * quarter:(MODES + 1) * quarter]
    partner_rows = partner_pack[:, :, (MODES + 1) * quarter:].reshape(
        subdomains, 4, MODES, coarse_total
    )

    opposite = jnp.array([1, 0, 3, 2], jnp.int32)
    offsets = (jnp.arange(4, dtype=jnp.int32) * quarter)[None, :, None]
    my_slot = maps.reshape(subdomains, 4, quarter) - offsets
    partner_slot = partner_map.astype(jnp.int32) - (opposite * quarter)[None, :, None]
    local = jnp.arange(quarter, dtype=jnp.int32)[None, None, None, :]
    mine_hot = (my_slot[..., None] == local).astype(jnp.bfloat16)
    partner_hot = (partner_slot[..., None] == local).astype(jnp.bfloat16)
    permutes = jnp.einsum(
        "sfmt,sfmi->sfti", partner_hot, mine_hot, preferred_element_type=jnp.float32
    )

    def to_mine(raw):
        return jnp.einsum("sfcq,sfqr->sfcr", raw, permutes, precision=HIGHEST)

    partner_modes = to_mine(partner_raw_modes)
    partner_slot_modes = jnp.moveaxis(partner_modes, 1, 2).reshape(subdomains, MODES, width)

    def partner_values(raw, shape):
        return jnp.moveaxis(to_mine(raw), 1, 2).reshape(shape)

    def jump(values):
        raw = neighbors(*face_split(values))
        return values - partner_values(raw, values.shape)

    def coefficients(values):
        return jnp.einsum("skm,snm->skn", weighted_modes, values, precision=HIGHEST)

    def gathered(coeffs, extra):
        payload = jnp.concatenate([coeffs.reshape(-1), extra.reshape(-1)])
        devices = lax.axis_size("grp") * lax.axis_size("sub")
        copies = jnp.broadcast_to(payload[None], (devices, payload.shape[0]))
        everything = lax.all_to_all(copies, ("grp", "sub"), 0, 0, tiled=True)
        count = coeffs.size
        extras = jnp.sum(everything[:, count:], axis=0)
        if count == 0:
            return None, extras
        flat = everything[:, :count].reshape(-1, columns)
        return flat, extras

    def lift(flat):
        amounts = jnp.dot(rows_here, flat, precision=HIGHEST, preferred_element_type=jnp.float32)
        shaped = amounts.reshape(subdomains, MODES, columns)
        far_amounts = jnp.einsum("sfkc,cn->skfn", partner_rows, flat, precision=HIGHEST)
        far_spread = jnp.repeat(jnp.swapaxes(far_amounts, 2, 3), quarter, axis=3)
        own_part = own_modes[:, :, None, :] * shaped[:, :, :, None]
        far_part = partner_slot_modes[:, :, None, :] * far_spread
        return jnp.sum(own_part - far_part, axis=1)

    def project_with(values, flat):
        return values - lift(flat)

    nothing = jnp.zeros((1,), jnp.float32)
    dual = vectors - partner_values(partner_gaps, vectors.shape)
    flat_dual, _ = gathered(coefficients(dual), nothing)
    residual = project_with(dual, flat_dual)
    flat_residual, _ = gathered(coefficients(residual), nothing)
    multipliers = jnp.zeros_like(dual)
    direction = jnp.zeros_like(dual)
    rho_prev = jnp.ones((columns,), jnp.float32)
    for step_index in range(ITERS):
        projected = project_with(residual, flat_residual)
        precond = jump(apply_blocks(projected, schur_blocks))
        flat_precond, rho_now = gathered(
            coefficients(precond), jnp.sum(projected * precond, axis=(0, 2))
        )
        search = project_with(precond, flat_precond)
        if step_index > 0:
            search = search + (rho_now / rho_prev)[None, :, None] * direction
        direction = search
        image = jump(apply_blocks(direction, stiffness))
        partial_dot = jnp.sum(direction * image, axis=(0, 2))
        if step_index + 1 < ITERS:
            flat_image, curvature = gathered(coefficients(image), partial_dot)
        else:
            _, curvature = gathered(jnp.zeros((0,), jnp.float32), partial_dot)
        step_len = rho_now / curvature
        multipliers = multipliers + step_len[None, :, None] * direction
        residual = residual - step_len[None, :, None] * image
        if step_index + 1 < ITERS:
            flat_residual = flat_residual - step_len[None, :] * flat_image
        rho_prev = rho_now
    return (multipliers[None], residual[None])


def solution(mesh):
    placed = (
        P("grp", "sub", None, None),
        P("grp", "sub", None, None),
        P("grp", "sub", None, None),
        P("grp", "sub", None, None),
        P("grp", "sub", None, None),
        P("grp", "sub", None),
    )
    return jax.shard_map(
        shards,
        mesh=mesh,
        in_specs=placed,
        out_specs=(P("grp", "sub", None, None), P("grp", "sub", None, None)),
        check_vma=False,
    )
```

```python
import jax
import jax.numpy as jnp
from jax import lax
from jax.sharding import PartitionSpec as P

MODES = 6
ITERS = 2


HIGHEST = lax.Precision.HIGHEST


def neighbors(d0, d1, d2, d3):
    sub_count = lax.axis_size("sub")
    grp_count = lax.axis_size("grp")
    up_sub = [(i, i + 1) for i in range(sub_count - 1)]
    down_sub = [(i + 1, i) for i in range(sub_count - 1)]
    up_grp = [(i, i + 1) for i in range(grp_count - 1)]
    down_grp = [(i + 1, i) for i in range(grp_count - 1)]
    left_dev = lax.ppermute(d1[-1:], "sub", up_sub)
    right_dev = lax.ppermute(d0[:1], "sub", down_sub)
    from_left = jnp.concatenate([left_dev, d1[:-1]], axis=0)
    from_right = jnp.concatenate([d0[1:], right_dev], axis=0)
    from_below = lax.ppermute(d3, "grp", up_grp)
    from_above = lax.ppermute(d2, "grp", down_grp)
    return jnp.stack([from_left, from_right, from_below, from_above], axis=1)


def face_split(values):
    quarter = values.shape[-1] // 4
    return [values[..., g * quarter:(g + 1) * quarter] for g in range(4)]


def apply_blocks(values, matrices):
    return jnp.einsum(
        "snm,smk->snk", values.astype(jnp.bfloat16), matrices, preferred_element_type=jnp.float32
    )


def shards(gaps, dual_op, dirichlet, modes, coarse_op, slot_map):
    maps = slot_map[0]
    vectors = gaps[0]
    stiffness = dual_op[0]
    schur_blocks = dirichlet[0]
    own_modes = modes[0]
    subdomains, columns, width = vectors.shape
    quarter = width // 4
    sub_total = lax.axis_size("sub")
    grp_total = lax.axis_size("grp")
    x_position = lax.axis_index("sub") * subdomains + jnp.arange(subdomains, dtype=jnp.int32)
    grp_here = lax.axis_index("grp")
    filler = jnp.ones((subdomains,), jnp.float32)
    face_weight = jnp.stack(
        [
            jnp.where(x_position == 0, 1.0, 2.0) * filler,
            jnp.where(x_position == sub_total * subdomains - 1, 1.0, 2.0) * filler,
            jnp.where(grp_here == 0, 1.0, 2.0) * filler,
            jnp.where(grp_here == grp_total - 1, 1.0, 2.0) * filler,
        ],
        axis=1,
    )
    slot_weight = jnp.repeat(face_weight, quarter, axis=1)
    weighted_modes = own_modes * slot_weight[:, None, :]
    rows_here = coarse_op[0].reshape(subdomains * MODES, -1)
    coarse_total = rows_here.shape[1]

    gap_faces = face_split(vectors)
    mode_faces = face_split(own_modes)
    map_faces = face_split(maps.astype(jnp.float32)[:, None, :])
    own_rows = coarse_op[0].reshape(subdomains, -1, quarter)
    packs = [
        jnp.concatenate([gap_faces[g], mode_faces[g], map_faces[g], own_rows], axis=1)
        for g in range(4)
    ]
    partner_pack = neighbors(*packs)
    partner_gaps = partner_pack[:, :, :columns]
    partner_raw_modes = partner_pack[:, :, columns:columns + MODES]
    partner_map = partner_pack[:, :, columns + MODES]
    partner_rows = partner_pack[:, :, columns + MODES + 1:].reshape(
        subdomains, 4, MODES, coarse_total
    )

    opposite = jnp.array([1, 0, 3, 2], jnp.int32)
    offsets = (jnp.arange(4, dtype=jnp.int32) * quarter)[None, :, None]
    my_slot = maps.reshape(subdomains, 4, quarter) - offsets
    partner_slot = partner_map.astype(jnp.int32) - (opposite * quarter)[None, :, None]
    local = jnp.arange(quarter, dtype=jnp.int32)[None, None, None, :]
    mine_hot = (my_slot[..., None] == local).astype(jnp.bfloat16)
    partner_hot = (partner_slot[..., None] == local).astype(jnp.bfloat16)
    permutes = jnp.einsum(
        "sfmt,sfmi->sfti", partner_hot, mine_hot, preferred_element_type=jnp.float32
    )

    def to_mine(raw):
        return jnp.einsum("sfcq,sfqr->sfcr", raw, permutes, precision=HIGHEST)

    partner_modes = to_mine(partner_raw_modes)
    partner_slot_modes = jnp.moveaxis(partner_modes, 1, 2).reshape(subdomains, MODES, width)

    def partner_values(raw, shape):
        return jnp.moveaxis(to_mine(raw), 1, 2).reshape(shape)

    def jump(values):
        raw = neighbors(*face_split(values))
        return values - partner_values(raw, values.shape)

    def coefficients(values):
        return jnp.einsum("skm,snm->skn", weighted_modes, values, precision=HIGHEST)

    def gathered(coeffs, extra):
        payload = jnp.concatenate([coeffs.reshape(-1), extra.reshape(-1)])
        devices = lax.axis_size("grp") * lax.axis_size("sub")
        copies = jnp.broadcast_to(payload[None], (devices, payload.shape[0]))
        everything = lax.all_to_all(copies, ("grp", "sub"), 0, 0, tiled=True)
        count = coeffs.size
        extras = jnp.sum(everything[:, count:], axis=0)
        if count == 0:
            return None, extras
        flat = everything[:, :count].reshape(-1, columns)
        return flat, extras

    def lift(flat):
        amounts = jnp.dot(rows_here, flat, precision=HIGHEST, preferred_element_type=jnp.float32)
        shaped = amounts.reshape(subdomains, MODES, columns)
        far_amounts = jnp.einsum("sfkc,cn->skfn", partner_rows, flat, precision=HIGHEST)
        far_spread = jnp.repeat(jnp.swapaxes(far_amounts, 2, 3), quarter, axis=3)
        own_part = own_modes[:, :, None, :] * shaped[:, :, :, None]
        far_part = partner_slot_modes[:, :, None, :] * far_spread
        return jnp.sum(own_part - far_part, axis=1)

    def project_with(values, flat):
        return values - lift(flat)

    nothing = jnp.zeros((1,), jnp.float32)
    dual = vectors - partner_values(partner_gaps, vectors.shape)
    flat_dual, _ = gathered(coefficients(dual), nothing)
    residual = project_with(dual, flat_dual)
    flat_residual, _ = gathered(coefficients(residual), nothing)
    multipliers = jnp.zeros_like(dual)
    direction = jnp.zeros_like(dual)
    rho_prev = jnp.ones((columns,), jnp.float32)
    for step_index in range(ITERS):
        projected = project_with(residual, flat_residual)
        precond = jump(apply_blocks(projected, schur_blocks))
        flat_precond, rho_now = gathered(
            coefficients(precond), jnp.sum(projected * precond, axis=(0, 2))
        )
        search = project_with(precond, flat_precond)
        if step_index > 0:
            search = search + (rho_now / rho_prev)[None, :, None] * direction
        direction = search
        image = jump(apply_blocks(direction, stiffness))
        partial_dot = jnp.sum(direction * image, axis=(0, 2))
        if step_index + 1 < ITERS:
            flat_image, curvature = gathered(coefficients(image), partial_dot)
        else:
            _, curvature = gathered(jnp.zeros((0,), jnp.float32), partial_dot)
        step_len = rho_now / curvature
        multipliers = multipliers + step_len[None, :, None] * direction
        residual = residual - step_len[None, :, None] * image
        if step_index + 1 < ITERS:
            flat_residual = flat_residual - step_len[None, :] * flat_image
        rho_prev = rho_now
    return (multipliers[None], residual[None])


def solution(mesh):
    placed = (
        P("grp", "sub", None, None),
        P("grp", "sub", None, None),
        P("grp", "sub", None, None),
        P("grp", "sub", None, None),
        P("grp", "sub", None, None),
        P("grp", "sub", None),
    )
    return jax.shard_map(
        shards,
        mesh=mesh,
        in_specs=placed,
        out_specs=(P("grp", "sub", None, None), P("grp", "sub", None, None)),
        check_vma=False,
    )
```

```python
import jax
import jax.numpy as jnp
from jax import lax
from jax.sharding import PartitionSpec as P

MODES = 6
ITERS = 2


HIGHEST = lax.Precision.HIGHEST


def neighbors(d0, d1, d2, d3):
    sub_count = lax.axis_size("sub")
    grp_count = lax.axis_size("grp")
    up_sub = [(i, i + 1) for i in range(sub_count - 1)]
    down_sub = [(i + 1, i) for i in range(sub_count - 1)]
    up_grp = [(i, i + 1) for i in range(grp_count - 1)]
    down_grp = [(i + 1, i) for i in range(grp_count - 1)]
    left_dev = lax.ppermute(d1[-1:], "sub", up_sub)
    right_dev = lax.ppermute(d0[:1], "sub", down_sub)
    from_left = jnp.concatenate([left_dev, d1[:-1]], axis=0)
    from_right = jnp.concatenate([d0[1:], right_dev], axis=0)
    from_below = lax.ppermute(d3, "grp", up_grp)
    from_above = lax.ppermute(d2, "grp", down_grp)
    return jnp.stack([from_left, from_right, from_below, from_above], axis=1)


def face_split(values):
    quarter = values.shape[-1] // 4
    return [values[..., g * quarter:(g + 1) * quarter] for g in range(4)]


def apply_blocks(values, matrices):
    return jnp.einsum(
        "snm,smk->snk", values.astype(jnp.bfloat16), matrices, preferred_element_type=jnp.float32
    )


def shards(gaps, dual_op, dirichlet, modes, coarse_op, slot_map):
    maps = slot_map[0]
    vectors = gaps[0]
    stiffness = dual_op[0]
    schur_blocks = dirichlet[0]
    own_modes = modes[0]
    subdomains, columns, width = vectors.shape
    quarter = width // 4
    sub_total = lax.axis_size("sub")
    grp_total = lax.axis_size("grp")
    x_position = lax.axis_index("sub") * subdomains + jnp.arange(subdomains, dtype=jnp.int32)
    grp_here = lax.axis_index("grp")
    filler = jnp.ones((subdomains,), jnp.float32)
    face_weight = jnp.stack(
        [
            jnp.where(x_position == 0, 1.0, 2.0) * filler,
            jnp.where(x_position == sub_total * subdomains - 1, 1.0, 2.0) * filler,
            jnp.where(grp_here == 0, 1.0, 2.0) * filler,
            jnp.where(grp_here == grp_total - 1, 1.0, 2.0) * filler,
        ],
        axis=1,
    )
    slot_weight = jnp.repeat(face_weight, quarter, axis=1)
    weighted_modes = own_modes * slot_weight[:, None, :]
    rows_here = coarse_op[0].reshape(subdomains * MODES, -1)
    coarse_total = rows_here.shape[1]

    gap_faces = face_split(vectors)
    mode_faces = face_split(own_modes)
    map_faces = face_split(maps.astype(jnp.float32)[:, None, :])
    own_rows = coarse_op[0].reshape(subdomains, -1, quarter)
    packs = [
        jnp.concatenate([gap_faces[g], mode_faces[g], map_faces[g], own_rows], axis=1)
        for g in range(4)
    ]
    partner_pack = neighbors(*packs)
    partner_gaps = partner_pack[:, :, :columns]
    partner_raw_modes = partner_pack[:, :, columns:columns + MODES]
    partner_map = partner_pack[:, :, columns + MODES]
    partner_rows = partner_pack[:, :, columns + MODES + 1:].reshape(
        subdomains, 4, MODES, coarse_total
    )

    opposite = jnp.array([1, 0, 3, 2], jnp.int32)
    offsets = (jnp.arange(4, dtype=jnp.int32) * quarter)[None, :, None]
    my_slot = maps.reshape(subdomains, 4, quarter) - offsets
    partner_slot = partner_map.astype(jnp.int32) - (opposite * quarter)[None, :, None]
    local = jnp.arange(quarter, dtype=jnp.int32)[None, None, None, :]
    mine_hot = (my_slot[..., None] == local).astype(jnp.bfloat16)
    partner_hot = (partner_slot[..., None] == local).astype(jnp.bfloat16)
    permutes = jnp.einsum(
        "sfmt,sfmi->sfti", partner_hot, mine_hot, preferred_element_type=jnp.float32
    )

    permutes_b = permutes.astype(jnp.bfloat16)

    def to_mine(raw):
        hi = raw.astype(jnp.bfloat16)
        rest = raw - hi.astype(jnp.float32)
        mid = rest.astype(jnp.bfloat16)
        lo = (rest - mid.astype(jnp.float32)).astype(jnp.bfloat16)

        def moved(part):
            return jnp.einsum(
                "sfcq,sfqr->sfcr", part, permutes_b, preferred_element_type=jnp.float32
            )

        return (moved(hi) + moved(mid)) + moved(lo)

    partner_modes = to_mine(partner_raw_modes)
    partner_slot_modes = jnp.moveaxis(partner_modes, 1, 2).reshape(subdomains, MODES, width)

    def partner_values(raw, shape):
        return jnp.moveaxis(to_mine(raw), 1, 2).reshape(shape)

    def jump(values):
        raw = neighbors(*face_split(values))
        return values - partner_values(raw, values.shape)

    def coefficients(values):
        return jnp.einsum("skm,snm->skn", weighted_modes, values, precision=HIGHEST)

    def gathered(coeffs, extra):
        payload = jnp.concatenate([coeffs.reshape(-1), extra.reshape(-1)])
        devices = lax.axis_size("grp") * lax.axis_size("sub")
        copies = jnp.broadcast_to(payload[None], (devices, payload.shape[0]))
        everything = lax.all_to_all(copies, ("grp", "sub"), 0, 0, tiled=True)
        count = coeffs.size
        extras = jnp.sum(everything[:, count:], axis=0)
        if count == 0:
            return None, extras
        flat = everything[:, :count].reshape(-1, columns)
        return flat, extras

    def lift(flat):
        amounts = jnp.dot(rows_here, flat, precision=HIGHEST, preferred_element_type=jnp.float32)
        shaped = amounts.reshape(subdomains, MODES, columns)
        far_amounts = jnp.einsum("sfkc,cn->skfn", partner_rows, flat, precision=HIGHEST)
        far_spread = jnp.repeat(jnp.swapaxes(far_amounts, 2, 3), quarter, axis=3)
        own_part = own_modes[:, :, None, :] * shaped[:, :, :, None]
        far_part = partner_slot_modes[:, :, None, :] * far_spread
        return jnp.sum(own_part - far_part, axis=1)

    def project_with(values, flat):
        return values - lift(flat)

    nothing = jnp.zeros((1,), jnp.float32)
    dual = vectors - partner_values(partner_gaps, vectors.shape)
    flat_dual, _ = gathered(coefficients(dual), nothing)
    residual = project_with(dual, flat_dual)
    flat_residual, _ = gathered(coefficients(residual), nothing)
    multipliers = jnp.zeros_like(dual)
    direction = jnp.zeros_like(dual)
    rho_prev = jnp.ones((columns,), jnp.float32)
    for step_index in range(ITERS):
        projected = project_with(residual, flat_residual)
        precond = jump(apply_blocks(projected, schur_blocks))
        flat_precond, rho_now = gathered(
            coefficients(precond), jnp.sum(projected * precond, axis=(0, 2))
        )
        search = project_with(precond, flat_precond)
        if step_index > 0:
            search = search + (rho_now / rho_prev)[None, :, None] * direction
        direction = search
        image = jump(apply_blocks(direction, stiffness))
        partial_dot = jnp.sum(direction * image, axis=(0, 2))
        if step_index + 1 < ITERS:
            flat_image, curvature = gathered(coefficients(image), partial_dot)
        else:
            _, curvature = gathered(jnp.zeros((0,), jnp.float32), partial_dot)
        step_len = rho_now / curvature
        multipliers = multipliers + step_len[None, :, None] * direction
        residual = residual - step_len[None, :, None] * image
        if step_index + 1 < ITERS:
            flat_residual = flat_residual - step_len[None, :] * flat_image
        rho_prev = rho_now
    return (multipliers[None], residual[None])


def solution(mesh):
    placed = (
        P("grp", "sub", None, None),
        P("grp", "sub", None, None),
        P("grp", "sub", None, None),
        P("grp", "sub", None, None),
        P("grp", "sub", None, None),
        P("grp", "sub", None),
    )
    return jax.shard_map(
        shards,
        mesh=mesh,
        in_specs=placed,
        out_specs=(P("grp", "sub", None, None), P("grp", "sub", None, None)),
        check_vma=False,
    )
```

```python
import jax
import jax.numpy as jnp
from jax import lax
from jax.sharding import PartitionSpec as P

MODES = 6
ITERS = 2


HIGHEST = lax.Precision.HIGHEST


def neighbors(d0, d1, d2, d3):
    sub_count = lax.axis_size("sub")
    grp_count = lax.axis_size("grp")
    up_sub = [(i, i + 1) for i in range(sub_count - 1)]
    down_sub = [(i + 1, i) for i in range(sub_count - 1)]
    up_grp = [(i, i + 1) for i in range(grp_count - 1)]
    down_grp = [(i + 1, i) for i in range(grp_count - 1)]
    left_dev = lax.ppermute(d1[-1:], "sub", up_sub)
    right_dev = lax.ppermute(d0[:1], "sub", down_sub)
    from_left = jnp.concatenate([left_dev, d1[:-1]], axis=0)
    from_right = jnp.concatenate([d0[1:], right_dev], axis=0)
    from_below = lax.ppermute(d3, "grp", up_grp)
    from_above = lax.ppermute(d2, "grp", down_grp)
    return jnp.stack([from_left, from_right, from_below, from_above], axis=1)


def face_split(values):
    quarter = values.shape[-1] // 4
    return [values[..., g * quarter:(g + 1) * quarter] for g in range(4)]


def apply_blocks(values, matrices):
    return jnp.einsum(
        "snm,smk->snk", values.astype(jnp.bfloat16), matrices, preferred_element_type=jnp.float32
    )


def shards(gaps, dual_op, dirichlet, modes, coarse_op, slot_map):
    maps = slot_map[0]
    vectors = gaps[0]
    stiffness = dual_op[0]
    schur_blocks = dirichlet[0]
    own_modes = modes[0]
    subdomains, columns, width = vectors.shape
    quarter = width // 4
    sub_total = lax.axis_size("sub")
    grp_total = lax.axis_size("grp")
    x_position = lax.axis_index("sub") * subdomains + jnp.arange(subdomains, dtype=jnp.int32)
    grp_here = lax.axis_index("grp")
    filler = jnp.ones((subdomains,), jnp.float32)
    face_weight = jnp.stack(
        [
            jnp.where(x_position == 0, 1.0, 2.0) * filler,
            jnp.where(x_position == sub_total * subdomains - 1, 1.0, 2.0) * filler,
            jnp.where(grp_here == 0, 1.0, 2.0) * filler,
            jnp.where(grp_here == grp_total - 1, 1.0, 2.0) * filler,
        ],
        axis=1,
    )
    slot_weight = jnp.repeat(face_weight, quarter, axis=1)
    weighted_modes = own_modes * slot_weight[:, None, :]
    rows_here = coarse_op[0].reshape(subdomains * MODES, -1)
    coarse_total = rows_here.shape[1]

    gap_faces = face_split(vectors)
    mode_faces = face_split(own_modes)
    map_faces = face_split(maps.astype(jnp.float32)[:, None, :])
    own_rows = coarse_op[0].reshape(subdomains, -1, quarter)
    packs = [
        jnp.concatenate([gap_faces[g], mode_faces[g], map_faces[g], own_rows], axis=1)
        for g in range(4)
    ]
    partner_pack = neighbors(*packs)
    partner_gaps = partner_pack[:, :, :columns]
    partner_raw_modes = partner_pack[:, :, columns:columns + MODES]
    partner_map = partner_pack[:, :, columns + MODES]
    partner_rows = partner_pack[:, :, columns + MODES + 1:].reshape(
        subdomains, 4, MODES, coarse_total
    )

    opposite = jnp.array([1, 0, 3, 2], jnp.int32)
    offsets = (jnp.arange(4, dtype=jnp.int32) * quarter)[None, :, None]
    my_slot = maps.reshape(subdomains, 4, quarter) - offsets
    partner_slot = partner_map.astype(jnp.int32) - (opposite * quarter)[None, :, None]
    local = jnp.arange(quarter, dtype=jnp.int32)[None, None, None, :]
    mine_hot = (my_slot[..., None] == local).astype(jnp.bfloat16)
    partner_hot = (partner_slot[..., None] == local).astype(jnp.bfloat16)
    permutes = jnp.einsum(
        "sfmt,sfmi->sfti", partner_hot, mine_hot, preferred_element_type=jnp.float32
    )

    def to_mine(raw):
        return jnp.einsum("sfcq,sfqr->sfcr", raw, permutes, precision=HIGHEST)

    partner_modes = to_mine(partner_raw_modes)
    partner_slot_modes = jnp.moveaxis(partner_modes, 1, 2).reshape(subdomains, MODES, width)

    def partner_values(raw, shape):
        return jnp.moveaxis(to_mine(raw), 1, 2).reshape(shape)

    def jump(values):
        raw = neighbors(*face_split(values))
        return values - partner_values(raw, values.shape)

    def coefficients(values):
        return jnp.einsum("skm,snm->skn", weighted_modes, values, precision=HIGHEST)

    def gathered(coeffs, extra):
        payload = jnp.concatenate([coeffs.reshape(-1), extra.reshape(-1)])
        devices = lax.axis_size("grp") * lax.axis_size("sub")
        copies = jnp.broadcast_to(payload[None], (devices, payload.shape[0]))
        everything = lax.all_to_all(copies, ("grp", "sub"), 0, 0, tiled=True)
        count = coeffs.size
        extras = jnp.sum(everything[:, count:], axis=0) if extra.size else None
        if count == 0:
            return None, extras
        flat = everything[:, :count].reshape(-1, columns)
        return flat, extras

    def lift(flat):
        amounts = jnp.dot(rows_here, flat, precision=HIGHEST, preferred_element_type=jnp.float32)
        shaped = amounts.reshape(subdomains, MODES, columns)
        far_amounts = jnp.einsum("sfkc,cn->skfn", partner_rows, flat, precision=HIGHEST)
        far_spread = jnp.repeat(jnp.swapaxes(far_amounts, 2, 3), quarter, axis=3)
        own_part = own_modes[:, :, None, :] * shaped[:, :, :, None]
        far_part = partner_slot_modes[:, :, None, :] * far_spread
        return jnp.sum(own_part - far_part, axis=1)

    def project_with(values, flat):
        return values - lift(flat)

    nothing = jnp.zeros((0,), jnp.float32)
    dual = vectors - partner_values(partner_gaps, vectors.shape)
    flat_dual, _ = gathered(coefficients(dual), nothing)
    residual = project_with(dual, flat_dual)
    flat_residual, _ = gathered(coefficients(residual), nothing)
    multipliers = jnp.zeros_like(dual)
    direction = jnp.zeros_like(dual)
    rho_prev = jnp.ones((columns,), jnp.float32)
    for step_index in range(ITERS):
        projected = project_with(residual, flat_residual)
        precond = jump(apply_blocks(projected, schur_blocks))
        flat_precond, rho_now = gathered(
            coefficients(precond), jnp.sum(projected * precond, axis=(0, 2))
        )
        search = project_with(precond, flat_precond)
        if step_index > 0:
            search = search + (rho_now / rho_prev)[None, :, None] * direction
        direction = search
        image = jump(apply_blocks(direction, stiffness))
        partial_dot = jnp.sum(direction * image, axis=(0, 2))
        if step_index + 1 < ITERS:
            flat_image, curvature = gathered(coefficients(image), partial_dot)
        else:
            _, curvature = gathered(jnp.zeros((0,), jnp.float32), partial_dot)
        step_len = rho_now / curvature
        multipliers = multipliers + step_len[None, :, None] * direction
        residual = residual - step_len[None, :, None] * image
        if step_index + 1 < ITERS:
            flat_residual = flat_residual - step_len[None, :] * flat_image
        rho_prev = rho_now
    return (multipliers[None], residual[None])


def solution(mesh):
    placed = (
        P("grp", "sub", None, None),
        P("grp", "sub", None, None),
        P("grp", "sub", None, None),
        P("grp", "sub", None, None),
        P("grp", "sub", None, None),
        P("grp", "sub", None),
    )
    return jax.shard_map(
        shards,
        mesh=mesh,
        in_specs=placed,
        out_specs=(P("grp", "sub", None, None), P("grp", "sub", None, None)),
        check_vma=False,
    )
```

```python
import jax
import jax.numpy as jnp
from jax import lax
from jax.sharding import PartitionSpec as P

MODES = 6
ITERS = 2


HIGHEST = lax.Precision.HIGHEST


def neighbors(d0, d1, d2, d3):
    sub_count = lax.axis_size("sub")
    grp_count = lax.axis_size("grp")
    up_sub = [(i, i + 1) for i in range(sub_count - 1)]
    down_sub = [(i + 1, i) for i in range(sub_count - 1)]
    up_grp = [(i, i + 1) for i in range(grp_count - 1)]
    down_grp = [(i + 1, i) for i in range(grp_count - 1)]
    left_dev = lax.ppermute(d1[-1:], "sub", up_sub)
    right_dev = lax.ppermute(d0[:1], "sub", down_sub)
    from_left = jnp.concatenate([left_dev, d1[:-1]], axis=0)
    from_right = jnp.concatenate([d0[1:], right_dev], axis=0)
    from_below = lax.ppermute(d3, "grp", up_grp)
    from_above = lax.ppermute(d2, "grp", down_grp)
    return jnp.stack([from_left, from_right, from_below, from_above], axis=1)


def face_split(values):
    quarter = values.shape[-1] // 4
    return [values[..., g * quarter:(g + 1) * quarter] for g in range(4)]


def apply_blocks(values, matrices):
    return jnp.einsum(
        "snm,smk->snk", values.astype(jnp.bfloat16), matrices, preferred_element_type=jnp.float32
    )


def shards(gaps, dual_op, dirichlet, modes, coarse_op, slot_map):
    maps = slot_map[0]
    vectors = gaps[0]
    stiffness = dual_op[0]
    schur_blocks = dirichlet[0]
    own_modes = modes[0]
    subdomains, columns, width = vectors.shape
    quarter = width // 4
    sub_total = lax.axis_size("sub")
    grp_total = lax.axis_size("grp")
    x_position = lax.axis_index("sub") * subdomains + jnp.arange(subdomains, dtype=jnp.int32)
    grp_here = lax.axis_index("grp")
    filler = jnp.ones((subdomains,), jnp.float32)
    face_weight = jnp.stack(
        [
            jnp.where(x_position == 0, 1.0, 2.0) * filler,
            jnp.where(x_position == sub_total * subdomains - 1, 1.0, 2.0) * filler,
            jnp.where(grp_here == 0, 1.0, 2.0) * filler,
            jnp.where(grp_here == grp_total - 1, 1.0, 2.0) * filler,
        ],
        axis=1,
    )
    slot_weight = jnp.repeat(face_weight, quarter, axis=1)
    weighted_modes = own_modes * slot_weight[:, None, :]
    rows_here = coarse_op[0].reshape(subdomains * MODES, -1)
    coarse_total = rows_here.shape[1]

    gap_faces = face_split(vectors)
    mode_faces = face_split(own_modes)
    map_faces = face_split(maps.astype(jnp.float32)[:, None, :])
    own_rows = coarse_op[0].reshape(subdomains, -1, quarter)
    packs = [
        jnp.concatenate([gap_faces[g], mode_faces[g], map_faces[g], own_rows], axis=1)
        for g in range(4)
    ]
    partner_pack = neighbors(*packs)
    partner_gaps = partner_pack[:, :, :columns]
    partner_raw_modes = partner_pack[:, :, columns:columns + MODES]
    partner_map = partner_pack[:, :, columns + MODES]
    partner_rows = partner_pack[:, :, columns + MODES + 1:].reshape(
        subdomains, 4, MODES, coarse_total
    )

    opposite = jnp.array([1, 0, 3, 2], jnp.int32)
    offsets = (jnp.arange(4, dtype=jnp.int32) * quarter)[None, :, None]
    my_slot = maps.reshape(subdomains, 4, quarter) - offsets
    partner_slot = partner_map.astype(jnp.int32) - (opposite * quarter)[None, :, None]
    local = jnp.arange(quarter, dtype=jnp.int32)[None, None, None, :]
    mine_hot = (my_slot[..., None] == local).astype(jnp.bfloat16)
    partner_hot = (partner_slot[..., None] == local).astype(jnp.bfloat16)
    permutes = jnp.einsum(
        "sfmt,sfmi->sfti", partner_hot, mine_hot, preferred_element_type=jnp.float32
    )

    def to_mine(raw):
        return jnp.einsum("sfcq,sfqr->sfcr", raw, permutes, precision=HIGHEST)

    partner_modes = to_mine(partner_raw_modes)
    partner_slot_modes = jnp.moveaxis(partner_modes, 1, 2).reshape(subdomains, MODES, width)

    def partner_values(raw, shape):
        return jnp.moveaxis(to_mine(raw), 1, 2).reshape(shape)

    def jump(values):
        raw = neighbors(*face_split(values))
        return values - partner_values(raw, values.shape)

    def coefficients(values):
        return jnp.einsum("skm,snm->skn", weighted_modes, values, precision=HIGHEST)

    def gathered(coeffs, extra):
        payload = jnp.concatenate([coeffs.reshape(-1), extra.reshape(-1)])
        devices = lax.axis_size("grp") * lax.axis_size("sub")
        copies = jnp.broadcast_to(payload[None], (devices, payload.shape[0]))
        everything = lax.all_to_all(copies, ("grp", "sub"), 0, 0, tiled=True)
        count = coeffs.size
        extras = jnp.sum(everything[:, count:], axis=0)
        if count == 0:
            return None, extras
        flat = everything[:, :count].reshape(-1, columns)
        return flat, extras

    def lift(flat):
        amounts = jnp.dot(rows_here, flat, precision=HIGHEST, preferred_element_type=jnp.float32)
        shaped = amounts.reshape(subdomains, MODES, columns)
        far_amounts = jnp.einsum("sfkc,cn->skfn", partner_rows, flat, precision=HIGHEST)
        far_spread = jnp.repeat(jnp.swapaxes(far_amounts, 2, 3), quarter, axis=3)
        own_part = own_modes[:, :, None, :] * shaped[:, :, :, None]
        far_part = partner_slot_modes[:, :, None, :] * far_spread
        return jnp.sum(own_part - far_part, axis=1)

    def project_with(values, flat):
        return values - lift(flat)

    nothing = jnp.zeros((1,), jnp.float32)
    dual = vectors - partner_values(partner_gaps, vectors.shape)
    flat_dual, _ = gathered(coefficients(dual), nothing)
    residual = project_with(dual, flat_dual)
    flat_residual, _ = gathered(coefficients(residual), nothing)
    multipliers = jnp.zeros_like(dual)
    direction = jnp.zeros_like(dual)
    rho_prev = jnp.ones((columns,), jnp.float32)
    for step_index in range(ITERS):
        projected = project_with(residual, flat_residual)
        precond = jump(apply_blocks(projected, schur_blocks))
        flat_precond, rho_now = gathered(
            coefficients(precond), jnp.sum(projected * precond, axis=(0, 2))
        )
        search = project_with(precond, flat_precond)
        if step_index > 0:
            search = search + (rho_now / rho_prev)[None, :, None] * direction
        direction = search
        if step_index + 1 < ITERS:
            image = jump(apply_blocks(direction, stiffness))
            partial_dot = jnp.sum(direction * image, axis=(0, 2))
            flat_image, curvature = gathered(coefficients(image), partial_dot)
        else:
            product = apply_blocks(direction, stiffness)
            partial_dot = jnp.sum(slot_weight[:, None, :] * direction * product, axis=(0, 2))
            _, curvature = gathered(jnp.zeros((0,), jnp.float32), partial_dot)
            image = jump(product)
        step_len = rho_now / curvature
        multipliers = multipliers + step_len[None, :, None] * direction
        residual = residual - step_len[None, :, None] * image
        if step_index + 1 < ITERS:
            flat_residual = flat_residual - step_len[None, :] * flat_image
        rho_prev = rho_now
    return (multipliers[None], residual[None])


def solution(mesh):
    placed = (
        P("grp", "sub", None, None),
        P("grp", "sub", None, None),
        P("grp", "sub", None, None),
        P("grp", "sub", None, None),
        P("grp", "sub", None, None),
        P("grp", "sub", None),
    )
    return jax.shard_map(
        shards,
        mesh=mesh,
        in_specs=placed,
        out_specs=(P("grp", "sub", None, None), P("grp", "sub", None, None)),
        check_vma=False,
    )
```

```python
import jax
import jax.numpy as jnp
from jax import lax
from jax.sharding import PartitionSpec as P

MODES = 6
ITERS = 2


HIGHEST = lax.Precision.HIGHEST


def neighbors(d0, d1, d2, d3):
    sub_count = lax.axis_size("sub")
    grp_count = lax.axis_size("grp")
    up_sub = [(i, i + 1) for i in range(sub_count - 1)]
    down_sub = [(i + 1, i) for i in range(sub_count - 1)]
    up_grp = [(i, i + 1) for i in range(grp_count - 1)]
    down_grp = [(i + 1, i) for i in range(grp_count - 1)]
    left_dev = lax.ppermute(d1[-1:], "sub", up_sub)
    right_dev = lax.ppermute(d0[:1], "sub", down_sub)
    from_left = jnp.concatenate([left_dev, d1[:-1]], axis=0)
    from_right = jnp.concatenate([d0[1:], right_dev], axis=0)
    from_below = lax.ppermute(d3, "grp", up_grp)
    from_above = lax.ppermute(d2, "grp", down_grp)
    return jnp.stack([from_left, from_right, from_below, from_above], axis=1)


def face_split(values):
    quarter = values.shape[-1] // 4
    return [values[..., g * quarter:(g + 1) * quarter] for g in range(4)]


def apply_blocks(values, matrices):
    return jnp.einsum(
        "snm,smk->snk", values.astype(jnp.bfloat16), matrices, preferred_element_type=jnp.float32
    )


def shards(gaps, dual_op, dirichlet, modes, coarse_op, slot_map):
    maps = slot_map[0]
    vectors = gaps[0]
    stiffness = dual_op[0]
    schur_blocks = dirichlet[0]
    own_modes = modes[0]
    subdomains, columns, width = vectors.shape
    quarter = width // 4
    sub_total = lax.axis_size("sub")
    grp_total = lax.axis_size("grp")
    x_position = lax.axis_index("sub") * subdomains + jnp.arange(subdomains, dtype=jnp.int32)
    grp_here = lax.axis_index("grp")
    filler = jnp.ones((subdomains,), jnp.float32)
    face_weight = jnp.stack(
        [
            jnp.where(x_position == 0, 1.0, 2.0) * filler,
            jnp.where(x_position == sub_total * subdomains - 1, 1.0, 2.0) * filler,
            jnp.where(grp_here == 0, 1.0, 2.0) * filler,
            jnp.where(grp_here == grp_total - 1, 1.0, 2.0) * filler,
        ],
        axis=1,
    )
    slot_weight = jnp.repeat(face_weight, quarter, axis=1)
    weighted_modes = own_modes * slot_weight[:, None, :]
    rows_here = coarse_op[0].reshape(subdomains * MODES, -1)
    coarse_total = rows_here.shape[1]

    gap_faces = face_split(vectors)
    mode_faces = face_split(own_modes)
    map_faces = face_split(maps.astype(jnp.float32)[:, None, :])
    own_rows = coarse_op[0].reshape(subdomains, -1, quarter)
    packs = [
        jnp.concatenate([gap_faces[g], mode_faces[g], map_faces[g], own_rows], axis=1)
        for g in range(4)
    ]
    partner_pack = neighbors(*packs)
    partner_gaps = partner_pack[:, :, :columns]
    partner_raw_modes = partner_pack[:, :, columns:columns + MODES]
    partner_map = partner_pack[:, :, columns + MODES]
    partner_rows = partner_pack[:, :, columns + MODES + 1:].reshape(
        subdomains, 4, MODES, coarse_total
    )

    opposite = jnp.array([1, 0, 3, 2], jnp.int32)
    offsets = (jnp.arange(4, dtype=jnp.int32) * quarter)[None, :, None]
    my_slot = maps.reshape(subdomains, 4, quarter) - offsets
    partner_slot = partner_map.astype(jnp.int32) - (opposite * quarter)[None, :, None]
    local = jnp.arange(quarter, dtype=jnp.int32)[None, None, None, :]
    mine_hot = (my_slot[..., None] == local).astype(jnp.bfloat16)
    partner_hot = (partner_slot[..., None] == local).astype(jnp.bfloat16)
    permutes = jnp.einsum(
        "sfmt,sfmi->sfti", partner_hot, mine_hot, preferred_element_type=jnp.float32
    )

    def to_mine(raw):
        return jnp.einsum("sfcq,sfqr->sfcr", raw, permutes, precision=HIGHEST)

    partner_modes = to_mine(partner_raw_modes)
    partner_slot_modes = jnp.moveaxis(partner_modes, 1, 2).reshape(subdomains, MODES, width)

    def partner_values(raw, shape):
        return jnp.moveaxis(to_mine(raw), 1, 2).reshape(shape)

    def jump(values):
        raw = neighbors(*face_split(values))
        return values - partner_values(raw, values.shape)

    def coefficients(values):
        return jnp.einsum("skm,snm->skn", weighted_modes, values, precision=HIGHEST)

    def gathered(coeffs, extra):
        payload = jnp.concatenate([coeffs.reshape(-1), extra.reshape(-1)])
        devices = lax.axis_size("grp") * lax.axis_size("sub")
        copies = jnp.broadcast_to(payload[None], (devices, payload.shape[0]))
        everything = lax.all_to_all(copies, ("grp", "sub"), 0, 0, tiled=True)
        count = coeffs.size
        extras = jnp.sum(everything[:, count:], axis=0)
        if count == 0:
            return None, extras
        flat = everything[:, :count].reshape(-1, columns)
        return flat, extras

    all_rows = jnp.concatenate([rows_here, partner_rows.reshape(-1, coarse_total)], axis=0)
    own_count = subdomains * MODES

    def lift(flat):
        both = jnp.dot(all_rows, flat, precision=HIGHEST, preferred_element_type=jnp.float32)
        shaped = both[:own_count].reshape(subdomains, MODES, columns)
        far_amounts = jnp.swapaxes(both[own_count:].reshape(subdomains, 4, MODES, columns), 1, 2)
        far_spread = jnp.repeat(jnp.swapaxes(far_amounts, 2, 3), quarter, axis=3)
        own_part = own_modes[:, :, None, :] * shaped[:, :, :, None]
        far_part = partner_slot_modes[:, :, None, :] * far_spread
        return jnp.sum(own_part - far_part, axis=1)

    def project_with(values, flat):
        return values - lift(flat)

    nothing = jnp.zeros((1,), jnp.float32)
    dual = vectors - partner_values(partner_gaps, vectors.shape)
    flat_dual, _ = gathered(coefficients(dual), nothing)
    residual = project_with(dual, flat_dual)
    flat_residual, _ = gathered(coefficients(residual), nothing)
    multipliers = jnp.zeros_like(dual)
    direction = jnp.zeros_like(dual)
    rho_prev = jnp.ones((columns,), jnp.float32)
    for step_index in range(ITERS):
        projected = project_with(residual, flat_residual)
        precond = jump(apply_blocks(projected, schur_blocks))
        flat_precond, rho_now = gathered(
            coefficients(precond), jnp.sum(projected * precond, axis=(0, 2))
        )
        search = project_with(precond, flat_precond)
        if step_index > 0:
            search = search + (rho_now / rho_prev)[None, :, None] * direction
        direction = search
        image = jump(apply_blocks(direction, stiffness))
        partial_dot = jnp.sum(direction * image, axis=(0, 2))
        if step_index + 1 < ITERS:
            flat_image, curvature = gathered(coefficients(image), partial_dot)
        else:
            _, curvature = gathered(jnp.zeros((0,), jnp.float32), partial_dot)
        step_len = rho_now / curvature
        multipliers = multipliers + step_len[None, :, None] * direction
        residual = residual - step_len[None, :, None] * image
        if step_index + 1 < ITERS:
            flat_residual = flat_residual - step_len[None, :] * flat_image
        rho_prev = rho_now
    return (multipliers[None], residual[None])


def solution(mesh):
    placed = (
        P("grp", "sub", None, None),
        P("grp", "sub", None, None),
        P("grp", "sub", None, None),
        P("grp", "sub", None, None),
        P("grp", "sub", None, None),
        P("grp", "sub", None),
    )
    return jax.shard_map(
        shards,
        mesh=mesh,
        in_specs=placed,
        out_specs=(P("grp", "sub", None, None), P("grp", "sub", None, None)),
        check_vma=False,
    )
```

```python
import jax
import jax.numpy as jnp
from jax import lax
from jax.sharding import PartitionSpec as P

MODES = 6
ITERS = 2


HIGHEST = lax.Precision.HIGHEST


def neighbors(d0, d1, d2, d3):
    return jnp.stack(neighbor_parts(d0, d1, d2, d3), axis=1)


def neighbor_parts(d0, d1, d2, d3):
    sub_count = lax.axis_size("sub")
    grp_count = lax.axis_size("grp")
    up_sub = [(i, i + 1) for i in range(sub_count - 1)]
    down_sub = [(i + 1, i) for i in range(sub_count - 1)]
    up_grp = [(i, i + 1) for i in range(grp_count - 1)]
    down_grp = [(i + 1, i) for i in range(grp_count - 1)]
    left_dev = lax.ppermute(d1[-1:], "sub", up_sub)
    right_dev = lax.ppermute(d0[:1], "sub", down_sub)
    from_left = jnp.concatenate([left_dev, d1[:-1]], axis=0)
    from_right = jnp.concatenate([d0[1:], right_dev], axis=0)
    from_below = lax.ppermute(d3, "grp", up_grp)
    from_above = lax.ppermute(d2, "grp", down_grp)
    return [from_left, from_right, from_below, from_above]


def face_split(values):
    quarter = values.shape[-1] // 4
    return [values[..., g * quarter:(g + 1) * quarter] for g in range(4)]


def apply_blocks(values, matrices):
    return jnp.einsum(
        "snm,smk->snk", values.astype(jnp.bfloat16), matrices, preferred_element_type=jnp.float32
    )


def shards(gaps, dual_op, dirichlet, modes, coarse_op, slot_map):
    maps = slot_map[0]
    vectors = gaps[0]
    stiffness = dual_op[0]
    schur_blocks = dirichlet[0]
    own_modes = modes[0]
    subdomains, columns, width = vectors.shape
    quarter = width // 4
    sub_total = lax.axis_size("sub")
    grp_total = lax.axis_size("grp")
    x_position = lax.axis_index("sub") * subdomains + jnp.arange(subdomains, dtype=jnp.int32)
    grp_here = lax.axis_index("grp")
    filler = jnp.ones((subdomains,), jnp.float32)
    face_weight = jnp.stack(
        [
            jnp.where(x_position == 0, 1.0, 2.0) * filler,
            jnp.where(x_position == sub_total * subdomains - 1, 1.0, 2.0) * filler,
            jnp.where(grp_here == 0, 1.0, 2.0) * filler,
            jnp.where(grp_here == grp_total - 1, 1.0, 2.0) * filler,
        ],
        axis=1,
    )
    slot_weight = jnp.repeat(face_weight, quarter, axis=1)
    weighted_modes = own_modes * slot_weight[:, None, :]
    rows_here = coarse_op[0].reshape(subdomains * MODES, -1)
    coarse_total = rows_here.shape[1]

    gap_faces = face_split(vectors)
    mode_faces = face_split(own_modes)
    map_faces = face_split(maps.astype(jnp.float32)[:, None, :])
    own_rows = coarse_op[0].reshape(subdomains, -1, quarter)
    packs = [
        jnp.concatenate([gap_faces[g], mode_faces[g], map_faces[g], own_rows], axis=1)
        for g in range(4)
    ]
    partner_pack = neighbors(*packs)
    partner_gaps = partner_pack[:, :, :columns]
    partner_raw_modes = partner_pack[:, :, columns:columns + MODES]
    partner_map = partner_pack[:, :, columns + MODES]
    partner_rows = partner_pack[:, :, columns + MODES + 1:].reshape(
        subdomains, 4, MODES, coarse_total
    )

    opposite = jnp.array([1, 0, 3, 2], jnp.int32)
    offsets = (jnp.arange(4, dtype=jnp.int32) * quarter)[None, :, None]
    my_slot = maps.reshape(subdomains, 4, quarter) - offsets
    partner_slot = partner_map.astype(jnp.int32) - (opposite * quarter)[None, :, None]
    local = jnp.arange(quarter, dtype=jnp.int32)[None, None, None, :]
    mine_hot = (my_slot[..., None] == local).astype(jnp.bfloat16)
    partner_hot = (partner_slot[..., None] == local).astype(jnp.bfloat16)
    permutes = jnp.einsum(
        "sfmt,sfmi->sfti", partner_hot, mine_hot, preferred_element_type=jnp.float32
    )

    def to_mine(raw):
        return jnp.einsum("sfcq,sfqr->sfcr", raw, permutes, precision=HIGHEST)

    partner_modes = to_mine(partner_raw_modes)
    partner_slot_modes = jnp.moveaxis(partner_modes, 1, 2).reshape(subdomains, MODES, width)

    def partner_values(raw, shape):
        return jnp.moveaxis(to_mine(raw), 1, 2).reshape(shape)

    def jump(values):
        parts = neighbor_parts(*face_split(values))
        beside = jnp.einsum(
            "sfcq,sfqr->sfcr", jnp.stack(parts[:2], axis=1), permutes[:, :2], precision=HIGHEST
        )
        across = jnp.einsum(
            "sfcq,sfqr->sfcr", jnp.stack(parts[2:], axis=1), permutes[:, 2:], precision=HIGHEST
        )
        partner = jnp.concatenate([beside, across], axis=1)
        return values - jnp.moveaxis(partner, 1, 2).reshape(values.shape)

    def coefficients(values):
        return jnp.einsum("skm,snm->skn", weighted_modes, values, precision=HIGHEST)

    def gathered(coeffs, extra):
        payload = jnp.concatenate([coeffs.reshape(-1), extra.reshape(-1)])
        devices = lax.axis_size("grp") * lax.axis_size("sub")
        copies = jnp.broadcast_to(payload[None], (devices, payload.shape[0]))
        everything = lax.all_to_all(copies, ("grp", "sub"), 0, 0, tiled=True)
        count = coeffs.size
        extras = jnp.sum(everything[:, count:], axis=0)
        if count == 0:
            return None, extras
        flat = everything[:, :count].reshape(-1, columns)
        return flat, extras

    def lift(flat):
        amounts = jnp.dot(rows_here, flat, precision=HIGHEST, preferred_element_type=jnp.float32)
        shaped = amounts.reshape(subdomains, MODES, columns)
        far_amounts = jnp.einsum("sfkc,cn->skfn", partner_rows, flat, precision=HIGHEST)
        far_spread = jnp.repeat(jnp.swapaxes(far_amounts, 2, 3), quarter, axis=3)
        own_part = own_modes[:, :, None, :] * shaped[:, :, :, None]
        far_part = partner_slot_modes[:, :, None, :] * far_spread
        return jnp.sum(own_part - far_part, axis=1)

    def project_with(values, flat):
        return values - lift(flat)

    nothing = jnp.zeros((1,), jnp.float32)
    dual = vectors - partner_values(partner_gaps, vectors.shape)
    flat_dual, _ = gathered(coefficients(dual), nothing)
    residual = project_with(dual, flat_dual)
    flat_residual, _ = gathered(coefficients(residual), nothing)
    multipliers = jnp.zeros_like(dual)
    direction = jnp.zeros_like(dual)
    rho_prev = jnp.ones((columns,), jnp.float32)
    for step_index in range(ITERS):
        projected = project_with(residual, flat_residual)
        precond = jump(apply_blocks(projected, schur_blocks))
        flat_precond, rho_now = gathered(
            coefficients(precond), jnp.sum(projected * precond, axis=(0, 2))
        )
        search = project_with(precond, flat_precond)
        if step_index > 0:
            search = search + (rho_now / rho_prev)[None, :, None] * direction
        direction = search
        image = jump(apply_blocks(direction, stiffness))
        partial_dot = jnp.sum(direction * image, axis=(0, 2))
        if step_index + 1 < ITERS:
            flat_image, curvature = gathered(coefficients(image), partial_dot)
        else:
            _, curvature = gathered(jnp.zeros((0,), jnp.float32), partial_dot)
        step_len = rho_now / curvature
        multipliers = multipliers + step_len[None, :, None] * direction
        residual = residual - step_len[None, :, None] * image
        if step_index + 1 < ITERS:
            flat_residual = flat_residual - step_len[None, :] * flat_image
        rho_prev = rho_now
    return (multipliers[None], residual[None])


def solution(mesh):
    placed = (
        P("grp", "sub", None, None),
        P("grp", "sub", None, None),
        P("grp", "sub", None, None),
        P("grp", "sub", None, None),
        P("grp", "sub", None, None),
        P("grp", "sub", None),
    )
    return jax.shard_map(
        shards,
        mesh=mesh,
        in_specs=placed,
        out_specs=(P("grp", "sub", None, None), P("grp", "sub", None, None)),
        check_vma=False,
    )
```

```python
import jax
import jax.numpy as jnp
from jax import lax
from jax.sharding import PartitionSpec as P

MODES = 6
ITERS = 2


HIGHEST = lax.Precision.HIGHEST


def neighbors(d0, d1, d2, d3):
    return jnp.stack(neighbor_parts(d0, d1, d2, d3), axis=1)


def neighbor_parts(d0, d1, d2, d3):
    sub_count = lax.axis_size("sub")
    grp_count = lax.axis_size("grp")
    up_sub = [(i, i + 1) for i in range(sub_count - 1)]
    down_sub = [(i + 1, i) for i in range(sub_count - 1)]
    up_grp = [(i, i + 1) for i in range(grp_count - 1)]
    down_grp = [(i + 1, i) for i in range(grp_count - 1)]
    left_dev = lax.ppermute(d1[-1:], "sub", up_sub)
    right_dev = lax.ppermute(d0[:1], "sub", down_sub)
    from_left = jnp.concatenate([left_dev, d1[:-1]], axis=0)
    from_right = jnp.concatenate([d0[1:], right_dev], axis=0)
    from_below = lax.ppermute(d3, "grp", up_grp)
    from_above = lax.ppermute(d2, "grp", down_grp)
    return [from_left, from_right, from_below, from_above]


def face_split(values):
    quarter = values.shape[-1] // 4
    return [values[..., g * quarter:(g + 1) * quarter] for g in range(4)]


def apply_blocks(values, matrices):
    return jnp.einsum(
        "snm,smk->snk", values.astype(jnp.bfloat16), matrices, preferred_element_type=jnp.float32
    )


def shards(gaps, dual_op, dirichlet, modes, coarse_op, slot_map):
    maps = slot_map[0]
    vectors = gaps[0]
    stiffness = dual_op[0]
    schur_blocks = dirichlet[0]
    own_modes = modes[0]
    subdomains, columns, width = vectors.shape
    quarter = width // 4
    sub_total = lax.axis_size("sub")
    grp_total = lax.axis_size("grp")
    x_position = lax.axis_index("sub") * subdomains + jnp.arange(subdomains, dtype=jnp.int32)
    grp_here = lax.axis_index("grp")
    filler = jnp.ones((subdomains,), jnp.float32)
    face_weight = jnp.stack(
        [
            jnp.where(x_position == 0, 1.0, 2.0) * filler,
            jnp.where(x_position == sub_total * subdomains - 1, 1.0, 2.0) * filler,
            jnp.where(grp_here == 0, 1.0, 2.0) * filler,
            jnp.where(grp_here == grp_total - 1, 1.0, 2.0) * filler,
        ],
        axis=1,
    )
    slot_weight = jnp.repeat(face_weight, quarter, axis=1)
    weighted_modes = own_modes * slot_weight[:, None, :]
    rows_here = coarse_op[0].reshape(subdomains * MODES, -1)
    coarse_total = rows_here.shape[1]

    gap_faces = face_split(vectors)
    mode_faces = face_split(own_modes)
    map_faces = face_split(maps.astype(jnp.float32)[:, None, :])
    own_rows = coarse_op[0].reshape(subdomains, -1, quarter)
    packs = [
        jnp.concatenate([gap_faces[g], mode_faces[g], map_faces[g], own_rows], axis=1)
        for g in range(4)
    ]
    pack_parts = neighbor_parts(*packs)

    opposite = jnp.array([1, 0, 3, 2], jnp.int32)
    offsets = (jnp.arange(4, dtype=jnp.int32) * quarter)[None, :, None]
    my_slot = maps.reshape(subdomains, 4, quarter) - offsets
    local = jnp.arange(quarter, dtype=jnp.int32)[None, None, None, :]
    mine_hot = (my_slot[..., None] == local).astype(jnp.bfloat16)

    def half_exchange(pieces, faces):
        pack = jnp.stack(pieces, axis=1)
        partner_map = pack[:, :, columns + MODES]
        partner_slot = partner_map.astype(jnp.int32) - (opposite[faces] * quarter)[None, :, None]
        partner_hot = (partner_slot[..., None] == local).astype(jnp.bfloat16)
        half_permutes = jnp.einsum(
            "sfmt,sfmi->sfti", partner_hot, mine_hot[:, faces], preferred_element_type=jnp.float32
        )
        gaps_half = jnp.einsum(
            "sfcq,sfqr->sfcr", pack[:, :, :columns], half_permutes, precision=HIGHEST
        )
        return pack, half_permutes, gaps_half

    pack_x, permutes_x, gaps_x = half_exchange(pack_parts[:2], slice(0, 2))
    pack_y, permutes_y, gaps_y = half_exchange(pack_parts[2:], slice(2, 4))
    partner_pack = jnp.concatenate([pack_x, pack_y], axis=1)
    permutes = jnp.concatenate([permutes_x, permutes_y], axis=1)
    partner_gaps_mine = jnp.concatenate([gaps_x, gaps_y], axis=1)
    partner_raw_modes = partner_pack[:, :, columns:columns + MODES]
    partner_rows = partner_pack[:, :, columns + MODES + 1:].reshape(
        subdomains, 4, MODES, coarse_total
    )

    def to_mine(raw):
        return jnp.einsum("sfcq,sfqr->sfcr", raw, permutes, precision=HIGHEST)

    partner_modes = to_mine(partner_raw_modes)
    partner_slot_modes = jnp.moveaxis(partner_modes, 1, 2).reshape(subdomains, MODES, width)

    def partner_values(raw, shape):
        return jnp.moveaxis(to_mine(raw), 1, 2).reshape(shape)

    def jump(values):
        parts = neighbor_parts(*face_split(values))
        beside = jnp.einsum(
            "sfcq,sfqr->sfcr", jnp.stack(parts[:2], axis=1), permutes[:, :2], precision=HIGHEST
        )
        across = jnp.einsum(
            "sfcq,sfqr->sfcr", jnp.stack(parts[2:], axis=1), permutes[:, 2:], precision=HIGHEST
        )
        partner = jnp.concatenate([beside, across], axis=1)
        return values - jnp.moveaxis(partner, 1, 2).reshape(values.shape)

    def coefficients(values):
        return jnp.einsum("skm,snm->skn", weighted_modes, values, precision=HIGHEST)

    def gathered(coeffs, extra):
        payload = jnp.concatenate([coeffs.reshape(-1), extra.reshape(-1)])
        devices = lax.axis_size("grp") * lax.axis_size("sub")
        copies = jnp.broadcast_to(payload[None], (devices, payload.shape[0]))
        everything = lax.all_to_all(copies, ("grp", "sub"), 0, 0, tiled=True)
        count = coeffs.size
        extras = jnp.sum(everything[:, count:], axis=0)
        if count == 0:
            return None, extras
        flat = everything[:, :count].reshape(-1, columns)
        return flat, extras

    def lift(flat):
        amounts = jnp.dot(rows_here, flat, precision=HIGHEST, preferred_element_type=jnp.float32)
        shaped = amounts.reshape(subdomains, MODES, columns)
        far_amounts = jnp.einsum("sfkc,cn->skfn", partner_rows, flat, precision=HIGHEST)
        far_spread = jnp.repeat(jnp.swapaxes(far_amounts, 2, 3), quarter, axis=3)
        own_part = own_modes[:, :, None, :] * shaped[:, :, :, None]
        far_part = partner_slot_modes[:, :, None, :] * far_spread
        return jnp.sum(own_part - far_part, axis=1)

    def project_with(values, flat):
        return values - lift(flat)

    nothing = jnp.zeros((1,), jnp.float32)
    dual = vectors - jnp.moveaxis(partner_gaps_mine, 1, 2).reshape(vectors.shape)
    flat_dual, _ = gathered(coefficients(dual), nothing)
    residual = project_with(dual, flat_dual)
    flat_residual, _ = gathered(coefficients(residual), nothing)
    multipliers = jnp.zeros_like(dual)
    direction = jnp.zeros_like(dual)
    rho_prev = jnp.ones((columns,), jnp.float32)
    for step_index in range(ITERS):
        projected = project_with(residual, flat_residual)
        precond = jump(apply_blocks(projected, schur_blocks))
        flat_precond, rho_now = gathered(
            coefficients(precond), jnp.sum(projected * precond, axis=(0, 2))
        )
        search = project_with(precond, flat_precond)
        if step_index > 0:
            search = search + (rho_now / rho_prev)[None, :, None] * direction
        direction = search
        image = jump(apply_blocks(direction, stiffness))
        partial_dot = jnp.sum(direction * image, axis=(0, 2))
        if step_index + 1 < ITERS:
            flat_image, curvature = gathered(coefficients(image), partial_dot)
        else:
            _, curvature = gathered(jnp.zeros((0,), jnp.float32), partial_dot)
        step_len = rho_now / curvature
        multipliers = multipliers + step_len[None, :, None] * direction
        residual = residual - step_len[None, :, None] * image
        if step_index + 1 < ITERS:
            flat_residual = flat_residual - step_len[None, :] * flat_image
        rho_prev = rho_now
    return (multipliers[None], residual[None])


def solution(mesh):
    placed = (
        P("grp", "sub", None, None),
        P("grp", "sub", None, None),
        P("grp", "sub", None, None),
        P("grp", "sub", None, None),
        P("grp", "sub", None, None),
        P("grp", "sub", None),
    )
    return jax.shard_map(
        shards,
        mesh=mesh,
        in_specs=placed,
        out_specs=(P("grp", "sub", None, None), P("grp", "sub", None, None)),
        check_vma=False,
    )
```

```python
import jax
import jax.numpy as jnp
from jax import lax
from jax.sharding import PartitionSpec as P

MODES = 6
ITERS = 2


HIGHEST = lax.Precision.HIGHEST


def neighbors(d0, d1, d2, d3):
    return jnp.stack(neighbor_parts(d0, d1, d2, d3), axis=1)


def neighbor_parts(d0, d1, d2, d3):
    sub_count = lax.axis_size("sub")
    grp_count = lax.axis_size("grp")
    up_sub = [(i, i + 1) for i in range(sub_count - 1)]
    down_sub = [(i + 1, i) for i in range(sub_count - 1)]
    up_grp = [(i, i + 1) for i in range(grp_count - 1)]
    down_grp = [(i + 1, i) for i in range(grp_count - 1)]
    left_dev = lax.ppermute(d1[-1:], "sub", up_sub)
    right_dev = lax.ppermute(d0[:1], "sub", down_sub)
    from_left = jnp.concatenate([left_dev, d1[:-1]], axis=0)
    from_right = jnp.concatenate([d0[1:], right_dev], axis=0)
    from_below = lax.ppermute(d3, "grp", up_grp)
    from_above = lax.ppermute(d2, "grp", down_grp)
    return [from_left, from_right, from_below, from_above]


def face_split(values):
    quarter = values.shape[-1] // 4
    return [values[..., g * quarter:(g + 1) * quarter] for g in range(4)]


def apply_blocks(values, matrices):
    return jnp.einsum(
        "snm,smk->snk", values.astype(jnp.bfloat16), matrices, preferred_element_type=jnp.float32
    )


def shards(gaps, dual_op, dirichlet, modes, coarse_op, slot_map):
    maps = slot_map[0]
    vectors = gaps[0]
    stiffness = dual_op[0]
    schur_blocks = dirichlet[0]
    own_modes = modes[0]
    subdomains, columns, width = vectors.shape
    quarter = width // 4
    sub_total = lax.axis_size("sub")
    grp_total = lax.axis_size("grp")
    x_position = lax.axis_index("sub") * subdomains + jnp.arange(subdomains, dtype=jnp.int32)
    grp_here = lax.axis_index("grp")
    filler = jnp.ones((subdomains,), jnp.float32)
    face_weight = jnp.stack(
        [
            jnp.where(x_position == 0, 1.0, 2.0) * filler,
            jnp.where(x_position == sub_total * subdomains - 1, 1.0, 2.0) * filler,
            jnp.where(grp_here == 0, 1.0, 2.0) * filler,
            jnp.where(grp_here == grp_total - 1, 1.0, 2.0) * filler,
        ],
        axis=1,
    )
    slot_weight = jnp.repeat(face_weight, quarter, axis=1)
    weighted_modes = own_modes * slot_weight[:, None, :]
    rows_here = coarse_op[0].reshape(subdomains * MODES, -1)
    coarse_total = rows_here.shape[1]

    gap_faces = face_split(vectors)
    mode_faces = face_split(own_modes)
    map_faces = face_split(maps.astype(jnp.float32)[:, None, :])
    own_rows = coarse_op[0].reshape(subdomains, -1, quarter)
    packs = [
        jnp.concatenate([gap_faces[g], mode_faces[g], map_faces[g], own_rows], axis=1)
        for g in range(4)
    ]
    pack_parts = neighbor_parts(*packs)

    opposite = jnp.array([1, 0, 3, 2], jnp.int32)
    offsets = (jnp.arange(4, dtype=jnp.int32) * quarter)[None, :, None]
    my_slot = maps.reshape(subdomains, 4, quarter) - offsets
    local = jnp.arange(quarter, dtype=jnp.int32)[None, None, None, :]
    mine_hot = (my_slot[..., None] == local).astype(jnp.bfloat16)

    def half_exchange(pieces, faces):
        pack = jnp.stack(pieces, axis=1)
        partner_map = pack[:, :, columns + MODES]
        partner_slot = partner_map.astype(jnp.int32) - (opposite[faces] * quarter)[None, :, None]
        partner_hot = (partner_slot[..., None] == local).astype(jnp.bfloat16)
        half_permutes = jnp.einsum(
            "sfmt,sfmi->sfti", partner_hot, mine_hot[:, faces], preferred_element_type=jnp.float32
        )
        moved = jnp.einsum(
            "sfcq,sfqr->sfcr", pack[:, :, :columns + MODES], half_permutes, precision=HIGHEST
        )
        return pack, half_permutes, moved

    pack_x, permutes_x, gaps_x = half_exchange(pack_parts[:2], slice(0, 2))
    pack_y, permutes_y, gaps_y = half_exchange(pack_parts[2:], slice(2, 4))
    partner_pack = jnp.concatenate([pack_x, pack_y], axis=1)
    permutes = jnp.concatenate([permutes_x, permutes_y], axis=1)
    moved_both = jnp.concatenate([gaps_x, gaps_y], axis=1)
    partner_gaps_mine = moved_both[:, :, :columns]
    partner_raw_modes = partner_pack[:, :, columns:columns + MODES]
    partner_rows = partner_pack[:, :, columns + MODES + 1:].reshape(
        subdomains, 4, MODES, coarse_total
    )

    def to_mine(raw):
        return jnp.einsum("sfcq,sfqr->sfcr", raw, permutes, precision=HIGHEST)

    partner_modes = moved_both[:, :, columns:columns + MODES]
    partner_slot_modes = jnp.moveaxis(partner_modes, 1, 2).reshape(subdomains, MODES, width)

    def partner_values(raw, shape):
        return jnp.moveaxis(to_mine(raw), 1, 2).reshape(shape)

    def jump(values):
        parts = neighbor_parts(*face_split(values))
        beside = jnp.einsum(
            "sfcq,sfqr->sfcr", jnp.stack(parts[:2], axis=1), permutes[:, :2], precision=HIGHEST
        )
        across = jnp.einsum(
            "sfcq,sfqr->sfcr", jnp.stack(parts[2:], axis=1), permutes[:, 2:], precision=HIGHEST
        )
        partner = jnp.concatenate([beside, across], axis=1)
        return values - jnp.moveaxis(partner, 1, 2).reshape(values.shape)

    def coefficients(values):
        return jnp.einsum("skm,snm->skn", weighted_modes, values, precision=HIGHEST)

    def gathered(coeffs, extra):
        payload = jnp.concatenate([coeffs.reshape(-1), extra.reshape(-1)])
        devices = lax.axis_size("grp") * lax.axis_size("sub")
        copies = jnp.broadcast_to(payload[None], (devices, payload.shape[0]))
        everything = lax.all_to_all(copies, ("grp", "sub"), 0, 0, tiled=True)
        count = coeffs.size
        extras = jnp.sum(everything[:, count:], axis=0)
        if count == 0:
            return None, extras
        flat = everything[:, :count].reshape(-1, columns)
        return flat, extras

    def lift(flat):
        amounts = jnp.dot(rows_here, flat, precision=HIGHEST, preferred_element_type=jnp.float32)
        shaped = amounts.reshape(subdomains, MODES, columns)
        far_amounts = jnp.einsum("sfkc,cn->skfn", partner_rows, flat, precision=HIGHEST)
        far_spread = jnp.repeat(jnp.swapaxes(far_amounts, 2, 3), quarter, axis=3)
        own_part = own_modes[:, :, None, :] * shaped[:, :, :, None]
        far_part = partner_slot_modes[:, :, None, :] * far_spread
        return jnp.sum(own_part - far_part, axis=1)

    def project_with(values, flat):
        return values - lift(flat)

    nothing = jnp.zeros((1,), jnp.float32)
    dual = vectors - jnp.moveaxis(partner_gaps_mine, 1, 2).reshape(vectors.shape)
    flat_dual, _ = gathered(coefficients(dual), nothing)
    residual = project_with(dual, flat_dual)
    flat_residual, _ = gathered(coefficients(residual), nothing)
    multipliers = jnp.zeros_like(dual)
    direction = jnp.zeros_like(dual)
    rho_prev = jnp.ones((columns,), jnp.float32)
    for step_index in range(ITERS):
        projected = project_with(residual, flat_residual)
        precond = jump(apply_blocks(projected, schur_blocks))
        flat_precond, rho_now = gathered(
            coefficients(precond), jnp.sum(projected * precond, axis=(0, 2))
        )
        search = project_with(precond, flat_precond)
        if step_index > 0:
            search = search + (rho_now / rho_prev)[None, :, None] * direction
        direction = search
        image = jump(apply_blocks(direction, stiffness))
        partial_dot = jnp.sum(direction * image, axis=(0, 2))
        if step_index + 1 < ITERS:
            flat_image, curvature = gathered(coefficients(image), partial_dot)
        else:
            _, curvature = gathered(jnp.zeros((0,), jnp.float32), partial_dot)
        step_len = rho_now / curvature
        multipliers = multipliers + step_len[None, :, None] * direction
        residual = residual - step_len[None, :, None] * image
        if step_index + 1 < ITERS:
            flat_residual = flat_residual - step_len[None, :] * flat_image
        rho_prev = rho_now
    return (multipliers[None], residual[None])


def solution(mesh):
    placed = (
        P("grp", "sub", None, None),
        P("grp", "sub", None, None),
        P("grp", "sub", None, None),
        P("grp", "sub", None, None),
        P("grp", "sub", None, None),
        P("grp", "sub", None),
    )
    return jax.shard_map(
        shards,
        mesh=mesh,
        in_specs=placed,
        out_specs=(P("grp", "sub", None, None), P("grp", "sub", None, None)),
        check_vma=False,
    )
```

```python
import jax
import jax.numpy as jnp
from jax import lax
from jax.sharding import PartitionSpec as P

MODES = 6
ITERS = 2


HIGHEST = lax.Precision.HIGHEST


def neighbors(d0, d1, d2, d3):
    return jnp.stack(neighbor_parts(d0, d1, d2, d3), axis=1)


def neighbor_parts(d0, d1, d2, d3):
    sub_count = lax.axis_size("sub")
    grp_count = lax.axis_size("grp")
    up_sub = [(i, i + 1) for i in range(sub_count - 1)]
    down_sub = [(i + 1, i) for i in range(sub_count - 1)]
    up_grp = [(i, i + 1) for i in range(grp_count - 1)]
    down_grp = [(i + 1, i) for i in range(grp_count - 1)]
    left_dev = lax.ppermute(d1[-1:], "sub", up_sub)
    right_dev = lax.ppermute(d0[:1], "sub", down_sub)
    from_left = jnp.concatenate([left_dev, d1[:-1]], axis=0)
    from_right = jnp.concatenate([d0[1:], right_dev], axis=0)
    from_below = lax.ppermute(d3, "grp", up_grp)
    from_above = lax.ppermute(d2, "grp", down_grp)
    return [from_left, from_right, from_below, from_above]


def face_split(values):
    quarter = values.shape[-1] // 4
    return [values[..., g * quarter:(g + 1) * quarter] for g in range(4)]


def apply_blocks(values, matrices):
    return jnp.einsum(
        "snm,smk->snk", values.astype(jnp.bfloat16), matrices, preferred_element_type=jnp.float32
    )


def shards(gaps, dual_op, dirichlet, modes, coarse_op, slot_map):
    maps = slot_map[0]
    vectors = gaps[0]
    stiffness = dual_op[0]
    schur_blocks = dirichlet[0]
    own_modes = modes[0]
    subdomains, columns, width = vectors.shape
    quarter = width // 4
    sub_total = lax.axis_size("sub")
    grp_total = lax.axis_size("grp")
    x_position = lax.axis_index("sub") * subdomains + jnp.arange(subdomains, dtype=jnp.int32)
    grp_here = lax.axis_index("grp")
    filler = jnp.ones((subdomains,), jnp.float32)
    face_weight = jnp.stack(
        [
            jnp.where(x_position == 0, 1.0, 2.0) * filler,
            jnp.where(x_position == sub_total * subdomains - 1, 1.0, 2.0) * filler,
            jnp.where(grp_here == 0, 1.0, 2.0) * filler,
            jnp.where(grp_here == grp_total - 1, 1.0, 2.0) * filler,
        ],
        axis=1,
    )
    slot_weight = jnp.repeat(face_weight, quarter, axis=1)
    weighted_modes = own_modes * slot_weight[:, None, :]
    rows_here = coarse_op[0].reshape(subdomains * MODES, -1)
    coarse_total = rows_here.shape[1]

    gap_faces = face_split(vectors)
    mode_faces = face_split(own_modes)
    map_faces = face_split(maps.astype(jnp.float32)[:, None, :])
    own_rows = coarse_op[0].reshape(subdomains, -1, quarter)
    packs = [
        jnp.concatenate([gap_faces[g], mode_faces[g], map_faces[g], own_rows], axis=1)
        for g in range(4)
    ]
    pack_parts = neighbor_parts(*packs)

    opposite = jnp.array([1, 0, 3, 2], jnp.int32)
    offsets = (jnp.arange(4, dtype=jnp.int32) * quarter)[None, :, None]
    my_slot = maps.reshape(subdomains, 4, quarter) - offsets
    local = jnp.arange(quarter, dtype=jnp.int32)[None, None, None, :]
    mine_hot = (my_slot[..., None] == local).astype(jnp.bfloat16)

    def half_exchange(pieces, faces):
        pack = jnp.stack(pieces, axis=1)
        partner_map = pack[:, :, columns + MODES]
        partner_slot = partner_map.astype(jnp.int32) - (opposite[faces] * quarter)[None, :, None]
        partner_hot = (partner_slot[..., None] == local).astype(jnp.bfloat16)
        half_permutes = jnp.einsum(
            "sfmt,sfmi->sfti", partner_hot, mine_hot[:, faces], preferred_element_type=jnp.float32
        )
        gaps_half = jnp.einsum(
            "sfcq,sfqr->sfcr", pack[:, :, :columns], half_permutes, precision=HIGHEST
        )
        return pack, half_permutes, gaps_half

    pack_x, permutes_x, gaps_x = half_exchange(pack_parts[:2], slice(0, 2))
    pack_y, permutes_y, gaps_y = half_exchange(pack_parts[2:], slice(2, 4))
    partner_pack = jnp.concatenate([pack_x, pack_y], axis=1)
    permutes = jnp.concatenate([permutes_x, permutes_y], axis=1)
    partner_gaps_mine = jnp.concatenate([gaps_x, gaps_y], axis=1)
    partner_raw_modes = partner_pack[:, :, columns:columns + MODES]
    partner_rows = partner_pack[:, :, columns + MODES + 1:].reshape(
        subdomains, 4, MODES, coarse_total
    )

    def to_mine(raw):
        return jnp.einsum("sfcq,sfqr->sfcr", raw, permutes, precision=HIGHEST)

    partner_modes = to_mine(partner_raw_modes)
    partner_slot_modes = jnp.moveaxis(partner_modes, 1, 2).reshape(subdomains, MODES, width)

    def partner_values(raw, shape):
        return jnp.moveaxis(to_mine(raw), 1, 2).reshape(shape)

    def jump(values):
        parts = neighbor_parts(*face_split(values))
        beside = jnp.einsum(
            "sfcq,sfqr->sfcr", jnp.stack(parts[:2], axis=1), permutes[:, :2], precision=HIGHEST
        )
        across = jnp.einsum(
            "sfcq,sfqr->sfcr", jnp.stack(parts[2:], axis=1), permutes[:, 2:], precision=HIGHEST
        )
        partner = jnp.concatenate([beside, across], axis=1)
        jumped = values - jnp.moveaxis(partner, 1, 2).reshape(values.shape)
        face_modes = weighted_modes.reshape(subdomains, MODES, 4, quarter)
        beside_coeffs = jnp.einsum(
            "skfq,sfnq->skn", face_modes[:, :, :2], beside, precision=HIGHEST
        )
        across_coeffs = jnp.einsum(
            "skfq,sfnq->skn", face_modes[:, :, 2:], across, precision=HIGHEST
        )
        return jumped, coefficients(values) - beside_coeffs - across_coeffs

    def coefficients(values):
        return jnp.einsum("skm,snm->skn", weighted_modes, values, precision=HIGHEST)

    def gathered(coeffs, extra):
        payload = jnp.concatenate([coeffs.reshape(-1), extra.reshape(-1)])
        devices = lax.axis_size("grp") * lax.axis_size("sub")
        copies = jnp.broadcast_to(payload[None], (devices, payload.shape[0]))
        everything = lax.all_to_all(copies, ("grp", "sub"), 0, 0, tiled=True)
        count = coeffs.size
        extras = jnp.sum(everything[:, count:], axis=0)
        if count == 0:
            return None, extras
        flat = everything[:, :count].reshape(-1, columns)
        return flat, extras

    def lift(flat):
        amounts = jnp.dot(rows_here, flat, precision=HIGHEST, preferred_element_type=jnp.float32)
        shaped = amounts.reshape(subdomains, MODES, columns)
        far_amounts = jnp.einsum("sfkc,cn->skfn", partner_rows, flat, precision=HIGHEST)
        far_spread = jnp.repeat(jnp.swapaxes(far_amounts, 2, 3), quarter, axis=3)
        own_part = own_modes[:, :, None, :] * shaped[:, :, :, None]
        far_part = partner_slot_modes[:, :, None, :] * far_spread
        return jnp.sum(own_part - far_part, axis=1)

    def project_with(values, flat):
        return values - lift(flat)

    nothing = jnp.zeros((1,), jnp.float32)
    dual = vectors - jnp.moveaxis(partner_gaps_mine, 1, 2).reshape(vectors.shape)
    flat_dual, _ = gathered(coefficients(dual), nothing)
    residual = project_with(dual, flat_dual)
    flat_residual, _ = gathered(coefficients(residual), nothing)
    multipliers = jnp.zeros_like(dual)
    direction = jnp.zeros_like(dual)
    rho_prev = jnp.ones((columns,), jnp.float32)
    for step_index in range(ITERS):
        projected = project_with(residual, flat_residual)
        precond, precond_coeffs = jump(apply_blocks(projected, schur_blocks))
        flat_precond, rho_now = gathered(
            precond_coeffs, jnp.sum(projected * precond, axis=(0, 2))
        )
        search = project_with(precond, flat_precond)
        if step_index > 0:
            search = search + (rho_now / rho_prev)[None, :, None] * direction
        direction = search
        image, image_coeffs = jump(apply_blocks(direction, stiffness))
        partial_dot = jnp.sum(direction * image, axis=(0, 2))
        if step_index + 1 < ITERS:
            flat_image, curvature = gathered(image_coeffs, partial_dot)
        else:
            _, curvature = gathered(jnp.zeros((0,), jnp.float32), partial_dot)
        step_len = rho_now / curvature
        multipliers = multipliers + step_len[None, :, None] * direction
        residual = residual - step_len[None, :, None] * image
        if step_index + 1 < ITERS:
            flat_residual = flat_residual - step_len[None, :] * flat_image
        rho_prev = rho_now
    return (multipliers[None], residual[None])


def solution(mesh):
    placed = (
        P("grp", "sub", None, None),
        P("grp", "sub", None, None),
        P("grp", "sub", None, None),
        P("grp", "sub", None, None),
        P("grp", "sub", None, None),
        P("grp", "sub", None),
    )
    return jax.shard_map(
        shards,
        mesh=mesh,
        in_specs=placed,
        out_specs=(P("grp", "sub", None, None), P("grp", "sub", None, None)),
        check_vma=False,
    )
```

```python
import jax
import jax.numpy as jnp
from jax import lax
from jax.sharding import PartitionSpec as P

MODES = 6
ITERS = 2


HIGHEST = lax.Precision.HIGHEST


def neighbors(d0, d1, d2, d3):
    return jnp.stack(neighbor_parts(d0, d1, d2, d3), axis=1)


def neighbor_parts(d0, d1, d2, d3):
    sub_count = lax.axis_size("sub")
    grp_count = lax.axis_size("grp")
    up_sub = [(i, i + 1) for i in range(sub_count - 1)]
    down_sub = [(i + 1, i) for i in range(sub_count - 1)]
    up_grp = [(i, i + 1) for i in range(grp_count - 1)]
    down_grp = [(i + 1, i) for i in range(grp_count - 1)]
    left_dev = lax.ppermute(d1[-1:], "sub", up_sub)
    right_dev = lax.ppermute(d0[:1], "sub", down_sub)
    from_left = jnp.concatenate([left_dev, d1[:-1]], axis=0)
    from_right = jnp.concatenate([d0[1:], right_dev], axis=0)
    from_below = lax.ppermute(d3, "grp", up_grp)
    from_above = lax.ppermute(d2, "grp", down_grp)
    return [from_left, from_right, from_below, from_above]


def face_split(values):
    quarter = values.shape[-1] // 4
    return [values[..., g * quarter:(g + 1) * quarter] for g in range(4)]


def apply_blocks(values, matrices):
    return jnp.einsum(
        "snm,smk->snk", values.astype(jnp.bfloat16), matrices, preferred_element_type=jnp.float32
    )


def shards(gaps, dual_op, dirichlet, modes, coarse_op, slot_map):
    maps = slot_map[0]
    vectors = gaps[0]
    stiffness = dual_op[0]
    schur_blocks = dirichlet[0]
    own_modes = modes[0]
    subdomains, columns, width = vectors.shape
    quarter = width // 4
    sub_total = lax.axis_size("sub")
    grp_total = lax.axis_size("grp")
    x_position = lax.axis_index("sub") * subdomains + jnp.arange(subdomains, dtype=jnp.int32)
    grp_here = lax.axis_index("grp")
    filler = jnp.ones((subdomains,), jnp.float32)
    face_weight = jnp.stack(
        [
            jnp.where(x_position == 0, 1.0, 2.0) * filler,
            jnp.where(x_position == sub_total * subdomains - 1, 1.0, 2.0) * filler,
            jnp.where(grp_here == 0, 1.0, 2.0) * filler,
            jnp.where(grp_here == grp_total - 1, 1.0, 2.0) * filler,
        ],
        axis=1,
    )
    slot_weight = jnp.repeat(face_weight, quarter, axis=1)
    weighted_modes = own_modes * slot_weight[:, None, :]
    rows_here = coarse_op[0].reshape(subdomains * MODES, -1)
    coarse_total = rows_here.shape[1]

    gap_faces = face_split(vectors)
    mode_faces = face_split(own_modes)
    map_faces = face_split(maps.astype(jnp.float32)[:, None, :])
    own_rows = coarse_op[0].reshape(subdomains, -1, quarter)
    packs = [
        jnp.concatenate([gap_faces[g], mode_faces[g], map_faces[g], own_rows], axis=1)
        for g in range(4)
    ]
    pack_parts = neighbor_parts(*packs)

    opposite = jnp.array([1, 0, 3, 2], jnp.int32)
    offsets = (jnp.arange(4, dtype=jnp.int32) * quarter)[None, :, None]
    my_slot = maps.reshape(subdomains, 4, quarter) - offsets
    local = jnp.arange(quarter, dtype=jnp.int32)[None, None, None, :]
    mine_hot = (my_slot[..., None] == local).astype(jnp.bfloat16)

    def half_exchange(pieces, faces):
        pack = jnp.stack(pieces, axis=1)
        partner_map = pack[:, :, columns + MODES]
        partner_slot = partner_map.astype(jnp.int32) - (opposite[faces] * quarter)[None, :, None]
        partner_hot = (partner_slot[..., None] == local).astype(jnp.bfloat16)
        half_permutes = jnp.einsum(
            "sfmt,sfmi->sfti", partner_hot, mine_hot[:, faces], preferred_element_type=jnp.float32
        )
        gaps_half = jnp.einsum(
            "sfcq,sfqr->sfcr", pack[:, :, :columns], half_permutes, precision=HIGHEST
        )
        return pack, half_permutes, gaps_half

    pack_x, permutes_x, gaps_x = half_exchange(pack_parts[:2], slice(0, 2))
    pack_y, permutes_y, gaps_y = half_exchange(pack_parts[2:], slice(2, 4))
    partner_pack = jnp.concatenate([pack_x, pack_y], axis=1)
    permutes = jnp.concatenate([permutes_x, permutes_y], axis=1)
    partner_gaps_mine = jnp.concatenate([gaps_x, gaps_y], axis=1)
    partner_raw_modes = partner_pack[:, :, columns:columns + MODES]
    partner_rows = partner_pack[:, :, columns + MODES + 1:].reshape(
        subdomains, 4, MODES, coarse_total
    )

    def to_mine(raw):
        return jnp.einsum("sfcq,sfqr->sfcr", raw, permutes, precision=HIGHEST)

    partner_modes = to_mine(partner_raw_modes)
    partner_slot_modes = jnp.moveaxis(partner_modes, 1, 2).reshape(subdomains, MODES, width)

    def partner_values(raw, shape):
        return jnp.moveaxis(to_mine(raw), 1, 2).reshape(shape)

    def jump(values):
        parts = neighbor_parts(*face_split(values))
        beside = jnp.einsum(
            "sfcq,sfqr->sfcr", jnp.stack(parts[:2], axis=1), permutes[:, :2], precision=HIGHEST
        )
        across = jnp.einsum(
            "sfcq,sfqr->sfcr", jnp.stack(parts[2:], axis=1), permutes[:, 2:], precision=HIGHEST
        )
        partner = jnp.concatenate([beside, across], axis=1)
        return values - jnp.moveaxis(partner, 1, 2).reshape(values.shape)

    def coefficients(values):
        return jnp.einsum("skm,snm->skn", weighted_modes, values, precision=HIGHEST)

    def gathered(coeffs, extra):
        payload = jnp.concatenate([coeffs.reshape(-1), extra.reshape(-1)])
        devices = lax.axis_size("grp") * lax.axis_size("sub")
        copies = jnp.broadcast_to(payload[None], (devices, payload.shape[0]))
        everything = lax.all_to_all(copies, ("grp", "sub"), 0, 0, tiled=True)
        count = coeffs.size
        extras = jnp.sum(everything[:, count:], axis=0)
        if count == 0:
            return None, extras
        flat = everything[:, :count].reshape(-1, columns)
        return flat, extras

    def lift(flat):
        amounts = jnp.dot(rows_here, flat, precision=HIGHEST, preferred_element_type=jnp.float32)
        shaped = amounts.reshape(subdomains, MODES, columns)
        far_amounts = jnp.einsum("sfkc,cn->skfn", partner_rows, flat, precision=HIGHEST)
        far_spread = jnp.repeat(jnp.swapaxes(far_amounts, 2, 3), quarter, axis=3)
        own_part = own_modes[:, :, None, :] * shaped[:, :, :, None]
        far_part = partner_slot_modes[:, :, None, :] * far_spread
        return jnp.sum(own_part - far_part, axis=1)

    def project_with(values, flat):
        return values - lift(flat)

    nothing = jnp.zeros((1,), jnp.float32)
    dual = vectors - jnp.moveaxis(partner_gaps_mine, 1, 2).reshape(vectors.shape)
    flat_dual, _ = gathered(coefficients(dual), nothing)
    residual = project_with(dual, flat_dual)
    flat_residual, _ = gathered(coefficients(residual), nothing)
    multipliers = jnp.zeros_like(dual)
    direction = jnp.zeros_like(dual)
    rho_prev = jnp.ones((columns,), jnp.float32)
    for step_index in range(ITERS):
        projected = project_with(residual, flat_residual)
        product = apply_blocks(projected, schur_blocks)
        rho_part = jnp.sum(slot_weight[:, None, :] * projected * product, axis=(0, 2))
        precond = jump(product)
        flat_precond, rho_now = gathered(coefficients(precond), rho_part)
        search = project_with(precond, flat_precond)
        if step_index > 0:
            search = search + (rho_now / rho_prev)[None, :, None] * direction
        direction = search
        product = apply_blocks(direction, stiffness)
        partial_dot = jnp.sum(slot_weight[:, None, :] * direction * product, axis=(0, 2))
        image = jump(product)
        if step_index + 1 < ITERS:
            flat_image, curvature = gathered(coefficients(image), partial_dot)
        else:
            _, curvature = gathered(jnp.zeros((0,), jnp.float32), partial_dot)
        step_len = rho_now / curvature
        multipliers = multipliers + step_len[None, :, None] * direction
        residual = residual - step_len[None, :, None] * image
        if step_index + 1 < ITERS:
            flat_residual = flat_residual - step_len[None, :] * flat_image
        rho_prev = rho_now
    return (multipliers[None], residual[None])


def solution(mesh):
    placed = (
        P("grp", "sub", None, None),
        P("grp", "sub", None, None),
        P("grp", "sub", None, None),
        P("grp", "sub", None, None),
        P("grp", "sub", None, None),
        P("grp", "sub", None),
    )
    return jax.shard_map(
        shards,
        mesh=mesh,
        in_specs=placed,
        out_specs=(P("grp", "sub", None, None), P("grp", "sub", None, None)),
        check_vma=False,
    )
```
